128 devices in a mesh: row: 4 (over y), col: 32 (over x, z, core).
Axes of the slice: x: 4, y: 4, z: 4, core: 2. Of those that a mesh axis runs over, the one named last changes fastest.
Arguments:
- depth: float32 [1024, 16384], P('row', 'col'), may hold values from 0.5 to 3
- bed: float32 [1024, 16384], P('row', 'col'), may hold values from -1 to 1
- mass: float32 [1024, 16384], P('row', 'col'), may hold values from 0.2 to 2
- conduct: float32 [1024, 16384], P('row', 'col'), may hold values from 0.02 to 0.2
- settle: float32 [1024, 16384], P('row', 'col'), may hold values from 0.02 to 0.5
- wet: int32 [1024, 16384], P('row', 'col'), may hold values 0 or 1
- link_block: int32 [65536], P(('row', 'col')), may hold values from 0 to 1023
- link_owner: int32 [65536, 1], P(('row', 'col')), may hold values from 0 to 127; in each aligned block of 512 rows (0 to 511, 512 to 1023, ...) at most 8 rows name the same one
- link_reach: int32 [65536], P(('row', 'col')), may hold values from 0 to 15
- link_coef: float32 [65536], P(('row', 'col')), may hold values from 0.05 to 0.5
- chan_phase: float32 [2048, 128], P(('row', 'col')), may hold values from -0.5 to 2
- chan_conc: float32 [2048, 128], P(('row', 'col')), may hold values from 0.1 to 1
- chan_area: float32 [2048, 128], P(('row', 'col')), may hold values from 2 to 20
Outputs:
- depth_out: float32 [1024, 16384], P('row', 'col')
- mass_out: float32 [1024, 16384], P('row', 'col')
- phase_out: float32 [2048, 128], P(('row', 'col'))
- conc_out: float32 [2048, 128], P(('row', 'col'))
The draws below stay inside these ranges and needn't reach their ends.
Inputs may be any that keep to these rules, and one draw needn't show every extreme that they name: `link_block`: block index within a tile. `link_owner`: among the 512 links of one tile, at most 8 name the same owner.
All inputs are finite; a program needn't handle non-finite values. No bound on the sum of `wet` on one device may be relied on, other than what follows from the above.
Results may differ from the reference program's by a relative error of at most 0.00005.
Values sent between devices are 32-bit elements; how exact they have to be, the bound alone decides.
No kernel may reach another device: no remote copies, remote signals or barrier semaphores. Data moves between devices by JAX's collectives and lax.ppermute only.
A program may use at most 64 MiB of HBM per device.

```python
import math
import jax
import jax.numpy as jnp
import numpy as np

TILE_Y = 256
TILE_X = 512
LINKS_DEV = 512
REACH_DEV = 16
SECTIONS = 128
CAP = 8
NY = 1024
NX = 16384
LINKS = 65536
REACHES = 2048
N_COL = 32
DEVICES = 128


def set_ends(values, rng, smallest, largest):
    place = [jax.random.randint(jax.random.fold_in(rng, axis), (), 0, length) for axis, length in enumerate(values.shape)]
    widest = values.shape.index(max(values.shape))
    neighbour = place[:widest] + [(place[widest] + 1) % values.shape[widest]] + place[widest + 1:]
    return values.at[tuple(place)].set(smallest).at[tuple(neighbour)].set(largest)


def block_levels(own_key, shape, cuts, smallest, top_value):
    loudness = 1.0
    for position, parts in cuts:
        heights = jax.random.uniform(jax.random.fold_in(jax.random.fold_in(own_key, 6), position), (parts,), jnp.float32, smallest / len(cuts), top_value / len(cuts))
        loudness = loudness * jnp.repeat(jnp.exp(heights), shape[position] // parts).reshape((-1,) + (1,) * (len(shape) - 1 - position))
    return loudness


def assign_block(rng, own, number, rows, amount, top, bound, lean):
    order = jax.random.permutation(rng, amount)
    packed, ordinary = shares(amount, rows * top, bound, lean, True), shares(amount, rows * top, bound, lean, False)
    places = jnp.arange(amount)

    def named(lengths, offset_by):
        used = int((lengths > 0).sum())
        fixed = max(1, used // 4)
        moved = fixed + (places - fixed + offset_by * (used - fixed)) % max(1, amount - fixed)
        return jnp.zeros((amount,), jnp.int32).at[order[jnp.where(places < fixed, places, moved)]].set(jnp.asarray(lengths, jnp.int32))

    lengths = jnp.where(number % 4 == 0, named(packed, number // 4), named(ordinary, number - number // 4 - 1))
    mixed = jax.random.permutation(jax.random.fold_in(own, 3), amount)
    donor, sink = mixed[0:amount // 2 * 2:2], mixed[1:amount // 2 * 2:2]
    room = jnp.minimum(lengths[donor] - 1, bound - lengths[sink]) // 2
    room = jnp.where((donor == order[0]) | (sink == order[0]) | (lengths[sink] == 0), 0, jnp.maximum(room, 0))
    moved = jax.random.randint(jax.random.fold_in(own, 4), (amount // 2,), 0, 1 << 20) % (room + 1)
    lengths = lengths.at[donor].add(-moved).at[sink].add(moved)
    labels = jnp.searchsorted(jnp.cumsum(lengths), jnp.arange(rows * top), side="right").astype(jnp.int32)
    grid = labels.reshape(top, rows).T
    grid = grid[jax.random.permutation(jax.random.fold_in(own, 1), rows)]
    offset_by = jax.random.randint(jax.random.fold_in(own, 2), (rows, 1), 0, top)
    return jnp.take_along_axis(grid, (jnp.arange(top)[None, :] + offset_by) % top, axis=1)


def shares(amount, total, most, lean, full):
    loads = [(1 << 20) // math.isqrt(grade ** lean) + 1 for grade in range(1, amount + 1)]
    largest = most if full else min(most, max(-(-total // amount), total * loads[0] // sum(loads)))
    least = 1 if total - largest >= amount - 1 else 0
    counts, rest = [largest] + [least] * (amount - 1), total - largest - least * (amount - 1)
    while rest > 0:
        candidates = [i for i in range(1, amount) if counts[i] < largest] or [i for i in range(1, amount) if counts[i] < most]
        pool, budget = sum([loads[i] for i in candidates]), rest
        for i in candidates:
            extra = min(most - counts[i], max(1, budget * loads[i] // pool), rest)
            counts[i] = counts[i] + extra
            rest = rest - extra
    return np.array(counts)


def setup_inputs(seed: int = 0) -> dict:
    splits = jax.random.split(jax.random.key(seed), 14)
    depth = jnp.clip(0.5 + 2.5 * jax.random.uniform(splits[0], (NY, NX), jnp.float32) ** block_levels(splits[0], (NY, NX), ((0, 4), (1, 32)), -0.2, 0.2), 0.5, 3.0)
    bed = jnp.clip(jax.random.uniform(splits[1], (NY, NX), jnp.float32, -1.0, 1.0) * block_levels(splits[1], (NY, NX), ((0, 4), (1, 32)), -0.4, 0.0), -1.0, 1.0)
    mass = jnp.clip(0.2 + 1.8 * jax.random.uniform(splits[2], (NY, NX), jnp.float32) ** block_levels(splits[2], (NY, NX), ((0, 4), (1, 32)), -0.2, 0.2), 0.2, 2.0)
    conduct = jnp.clip(jnp.exp(math.log(0.2) - 2.3025851 * jax.random.uniform(splits[3], (NY, NX), jnp.float32) ** block_levels(splits[3], (NY, NX), ((0, 4), (1, 32)), -0.2, 0.2)), 0.02, 0.2)
    settle = jnp.clip(jnp.exp(math.log(0.5) - 3.218876 * jax.random.uniform(splits[4], (NY, NX), jnp.float32) ** block_levels(splits[4], (NY, NX), ((0, 4), (1, 32)), -0.2, 0.2)), 0.02, 0.5)
    wet = set_ends((jax.random.randint(splits[5], (NY, NX), 0, 4) < 3).astype(jnp.int32), jax.random.fold_in(splits[5], 1), 0, 1)
    link_block = set_ends(jax.random.randint(splits[6], (LINKS,), 0, TILE_Y * TILE_X // 128), jax.random.fold_in(splits[6], 1), 0, (TILE_Y * TILE_X // 128) - 1).astype(jnp.int32)
    link_owner_keys = jax.random.split(jax.random.fold_in(splits[7], 1), LINKS // LINKS_DEV)
    link_owner_turns = jax.random.permutation(jax.random.fold_in(splits[7], 3), LINKS // LINKS_DEV)
    link_owner = jax.vmap(lambda own, number: assign_block(jax.random.fold_in(splits[7], 2), own, number, LINKS_DEV, DEVICES, 1, CAP, 2))(link_owner_keys, link_owner_turns).reshape((LINKS, 1))
    link_reach = set_ends(jax.random.randint(splits[8], (LINKS,), 0, REACH_DEV), jax.random.fold_in(splits[8], 1), 0, REACH_DEV - 1).astype(jnp.int32)
    link_coef = jnp.clip(jnp.exp(math.log(0.5) - 2.3025851 * jax.random.uniform(splits[9], (LINKS,), jnp.float32) ** block_levels(splits[9], (LINKS,), ((0, 128),), -0.2, 0.2)), 0.05, 0.5)
    chan_phase = jnp.clip(-0.5 + 2.5 * jax.random.uniform(splits[10], (REACHES, SECTIONS), jnp.float32) ** block_levels(splits[10], (REACHES, SECTIONS), ((0, 128),), -0.2, 0.2), -0.5, 2.0)
    chan_conc = jnp.clip(0.1 + 0.9 * jax.random.uniform(splits[11], (REACHES, SECTIONS), jnp.float32) ** block_levels(splits[11], (REACHES, SECTIONS), ((0, 128),), -0.2, 0.2), 0.1, 1.0)
    chan_area = jnp.clip(jnp.exp(math.log(20.0) - 2.3025851 * jax.random.uniform(splits[12], (REACHES, SECTIONS), jnp.float32) ** block_levels(splits[12], (REACHES, SECTIONS), ((0, 128),), -0.2, 0.2)), 2.0, 20.0)
    return dict(depth=depth, bed=bed, mass=mass, conduct=conduct, settle=settle, wet=wet, link_block=link_block, link_owner=link_owner, link_reach=link_reach, link_coef=link_coef, chan_phase=chan_phase, chan_conc=chan_conc, chan_area=chan_area)


def shifted(padded, step_y, step_x, size_y, size_x):
    return padded[1 + step_y:1 + step_y + size_y, 1 + step_x:1 + step_x + size_x]


def smooth_reach(values):
    left = jnp.concatenate([values[:, :1], values[:, :-1]], axis=1)
    right = jnp.concatenate([values[:, 1:], values[:, -1:]], axis=1)
    return values + 0.25 * (left - 2.0 * values + right)


def reference(depth, bed, mass, conduct, settle, wet, link_block, link_owner, link_reach, link_coef, chan_phase, chan_conc, chan_area):
    size_y, size_x = depth.shape
    surface = depth + bed
    opened = wet.astype(jnp.float32)
    pad_surf = jnp.pad(surface, 1)
    pad_mass = jnp.pad(mass, 1)
    pad_cond = jnp.pad(conduct, 1)
    pad_open = jnp.pad(opened, 1)
    water_gain = jnp.zeros_like(depth)
    mass_gain = jnp.zeros_like(depth)
    for step_y, step_x in ((1, 0), (-1, 0), (0, 1), (0, -1)):
        coeff = 0.5 * (conduct + shifted(pad_cond, step_y, step_x, size_y, size_x)) * opened * shifted(pad_open, step_y, step_x, size_y, size_x)
        water_gain = water_gain + coeff * (shifted(pad_surf, step_y, step_x, size_y, size_x) - surface)
        mass_gain = mass_gain + coeff * (shifted(pad_mass, step_y, step_x, size_y, size_x) - mass)
    depth1 = depth + water_gain
    mass1 = (mass + mass_gain) * jnp.exp(-settle)
    surface1 = depth1 + bed
    link_ids = jnp.arange(LINKS, dtype=jnp.int32)
    tile_ids = link_ids // LINKS_DEV
    tile_row = tile_ids // N_COL
    tile_col = tile_ids % N_COL
    per_row = TILE_X // 128
    cell_y = tile_row * TILE_Y + link_block // per_row
    cell_x0 = tile_col * TILE_X + (link_block % per_row) * 128
    cell_xs = cell_x0[:, None] + jnp.arange(128, dtype=jnp.int32)[None, :]
    cell_ys = jnp.broadcast_to(cell_y[:, None], cell_xs.shape)
    weight = link_coef[:, None] * opened[cell_ys, cell_xs]
    surf_rows = surface1[cell_ys, cell_xs]
    mass_rows = mass1[cell_ys, cell_xs]
    reach_ids = (link_owner[:, 0] * REACH_DEV + link_reach).astype(jnp.int32)
    inflow = jax.ops.segment_sum(weight * surf_rows, reach_ids, num_segments=REACHES)
    wet_sum = jax.ops.segment_sum(weight, reach_ids, num_segments=REACHES)
    sediment = jax.ops.segment_sum(weight * mass_rows, reach_ids, num_segments=REACHES)
    phase_new = (chan_area * chan_phase + inflow) / (chan_area + wet_sum)
    conc_new = (chan_area * chan_conc + sediment) / (chan_area + wet_sum)
    phase_out = smooth_reach(phase_new)
    conc_out = smooth_reach(conc_new)
    depth_out = depth1.at[cell_ys, cell_xs].add(0.5 * weight * (phase_out[reach_ids] - surf_rows))
    mass_out = mass1.at[cell_ys, cell_xs].add(0.5 * weight * (conc_out[reach_ids] - mass_rows))
    return depth_out, mass_out, phase_out, conc_out
```

```python
import jax
import jax.numpy as jnp
from jax import lax
from jax.experimental import pallas as pl
from jax.experimental.pallas import tpu as pltpu
from jax.sharding import PartitionSpec as P


def halo(fields, axis, dim):
    count = lax.axis_size(axis)
    forward = [(i, i + 1) for i in range(count - 1)]
    backward = [(target, source) for source, target in forward]
    size = fields.shape[dim]
    low = lax.ppermute(lax.index_in_dim(fields, size - 1, axis=dim, keepdims=False), axis, forward)
    high = lax.ppermute(lax.index_in_dim(fields, 0, axis=dim, keepdims=False), axis, backward)
    return low, high


def stencil_kernel(depth_ref, bed_ref, mass_ref, cond_ref, settle_ref, wet_ref, rows_ref, cols_ref,
                   depth1_ref, mass1_ref, surf1_ref):
    depth = depth_ref[...]
    bed = bed_ref[...]
    mass = mass_ref[...]
    cond = cond_ref[...]
    opened = wet_ref[...].astype(jnp.float32)
    surface = depth + bed
    tile_y, tile_x = depth.shape
    own = (surface, mass, cond, opened)
    row_id = lax.broadcasted_iota(jnp.int32, (tile_y, tile_x), 0)
    col_id = lax.broadcasted_iota(jnp.int32, (tile_y, tile_x), 1)
    rows = rows_ref[...]
    cols = cols_ref[...]

    def neighbour(field, step_y, step_x):
        value = own[field]
        if step_y == 1:
            edge = rows[4 + field : 5 + field, :]
            return jnp.where(row_id == tile_y - 1, edge, pltpu.roll(value, tile_y - 1, 0))
        if step_y == -1:
            edge = rows[field : field + 1, :]
            return jnp.where(row_id == 0, edge, pltpu.roll(value, 1, 0))
        if step_x == 1:
            edge = cols[:, 4 + field : 5 + field]
            return jnp.where(col_id == tile_x - 1, edge, pltpu.roll(value, tile_x - 1, 1))
        edge = cols[:, field : field + 1]
        return jnp.where(col_id == 0, edge, pltpu.roll(value, 1, 1))

    water_gain = jnp.zeros_like(depth)
    mass_gain = jnp.zeros_like(depth)
    for step_y, step_x in ((1, 0), (-1, 0), (0, 1), (0, -1)):
        coeff = 0.5 * (cond + neighbour(2, step_y, step_x)) * opened * neighbour(3, step_y, step_x)
        water_gain = water_gain + coeff * (neighbour(0, step_y, step_x) - surface)
        mass_gain = mass_gain + coeff * (neighbour(1, step_y, step_x) - mass)
    depth1 = depth + water_gain
    depth1_ref[...] = depth1
    mass1_ref[...] = (mass + mass_gain) * jnp.exp(-settle_ref[...])
    surf1_ref[...] = depth1 + bed


def smooth_reach(values):
    left = jnp.concatenate([values[:, :1], values[:, :-1]], axis=1)
    right = jnp.concatenate([values[:, 1:], values[:, -1:]], axis=1)
    return values + 0.25 * (left - 2.0 * values + right)


def body(
    depth,
    bed,
    mass,
    conduct,
    settle,
    wet,
    link_block,
    link_owner,
    link_reach,
    link_coef,
    chan_phase,
    chan_conc,
    chan_area,
):
    tile_y, tile_x = depth.shape
    opened = wet.astype(jnp.float32)
    surface = depth + bed
    stacked = jnp.stack([surface, mass, conduct, opened])
    top, bottom = halo(stacked, "row", 1)
    left, right = halo(stacked, "col", 2)
    rows = jnp.concatenate([top, bottom], axis=0)
    cols = jnp.concatenate([left, right], axis=0).T
    tile = jax.ShapeDtypeStruct((tile_y, tile_x), jnp.float32)
    vmem = pl.BlockSpec(memory_space=pltpu.VMEM)
    depth1, mass1, surface1 = pl.pallas_call(
        stencil_kernel,
        out_shape=[tile, tile, tile],
        in_specs=[vmem] * 8,
        out_specs=[vmem] * 3,
        cost_estimate=pl.CostEstimate(
            flops=60 * tile_y * tile_x, transcendentals=tile_y * tile_x, bytes_accessed=36 * tile_y * tile_x
        ),
    )(depth, bed, mass, conduct, settle, wet, rows, cols)

    blocks = tile_y * tile_x // 128
    surf_rows = surface1.reshape(blocks, 128)[link_block]
    mass_rows = mass1.reshape(blocks, 128)[link_block]
    weight = link_coef[:, None] * opened.reshape(blocks, 128)[link_block]
    ws = weight * surf_rows
    wm = weight * mass_rows

    n_row = lax.axis_size("row")
    n_col = lax.axis_size("col")
    devices = n_row * n_col
    links_here = link_owner.shape[0]
    slot_cap = max(2, 2 * links_here // devices)
    target = link_owner[:, 0]
    owner_hot = (target[:, None] == jnp.arange(devices, dtype=jnp.int32)[None, :]).astype(jnp.int32)
    ranking = jnp.sum((jnp.cumsum(owner_hot, axis=0) - 1) * owner_hot, axis=1)
    slot_of = target * slot_cap + ranking
    slot_ids = jnp.arange(devices * slot_cap, dtype=jnp.int32)
    slot_hit = slot_of[None, :] == slot_ids[:, None]
    link_ids = jnp.arange(links_here, dtype=jnp.int32)
    filler = jnp.max(jnp.where(slot_hit, link_ids[None, :], -1), axis=1)
    used = filler >= 0
    source = jnp.maximum(filler, 0)
    payload = jnp.where(used[:, None, None], jnp.stack([ws, wm], axis=1)[source], 0.0)
    tags = jnp.where(used, link_reach[source].astype(jnp.float32), -1.0)
    coefs = jnp.where(used, link_coef[source], 0.0)
    meta = jnp.concatenate(
        [tags.reshape(devices, slot_cap), coefs.reshape(devices, slot_cap),
         jnp.zeros((devices, 128 - 2 * slot_cap), jnp.float32)],
        axis=1,
    )
    outgoing = jnp.concatenate(
        [payload.reshape(devices, 2 * slot_cap, 128), meta[:, None, :]], axis=1
    )
    arrived = lax.all_to_all(outgoing, ("row", "col"), split_axis=0, concat_axis=0, tiled=True)
    got = arrived[:, : 2 * slot_cap, :].reshape(devices * slot_cap, 2, 128)
    arrived_tags = arrived[:, 2 * slot_cap, :slot_cap].reshape(devices * slot_cap)
    arrived_coef = arrived[:, 2 * slot_cap, slot_cap : 2 * slot_cap].reshape(devices * slot_cap)
    got_ws = got[:, 0, :]
    got_wm = got[:, 1, :]
    got_w = jnp.where(got_wm > 0.0, arrived_coef[:, None], 0.0)
    reach_dev = chan_phase.shape[0]
    reach_hot = (arrived_tags[None, :] == jnp.arange(reach_dev, dtype=jnp.float32)[:, None]).astype(
        jnp.float32
    )
    totals = jnp.dot(
        reach_hot, jnp.concatenate([got_ws, got_wm, got_w], axis=1), precision=lax.Precision.HIGHEST
    )
    inflow = totals[:, :128]
    sediment = totals[:, 128:256]
    wet_sum = totals[:, 256:]
    phase_new = (chan_area * chan_phase + inflow) / (chan_area + wet_sum)
    conc_new = (chan_area * chan_conc + sediment) / (chan_area + wet_sum)
    phase_out = smooth_reach(phase_new)
    conc_out = smooth_reach(conc_new)
    reply = jnp.dot(
        reach_hot.T, jnp.concatenate([phase_out, conc_out], axis=1), precision=lax.Precision.HIGHEST
    )
    answered = lax.all_to_all(
        reply.reshape(devices, slot_cap * 2, 128),
        ("row", "col"),
        split_axis=0,
        concat_axis=0,
        tiled=True,
    )
    own_rows = answered.reshape(devices * slot_cap, 256)[slot_of]
    applied = jnp.concatenate(
        [
            0.5 * weight * (own_rows[:, :128] - surf_rows),
            0.5 * weight * (own_rows[:, 128:] - mass_rows),
        ],
        axis=1,
    )
    block_hot = (jnp.arange(blocks, dtype=jnp.int32)[:, None] == link_block[None, :]).astype(
        jnp.float32
    )
    gained = jnp.dot(block_hot, applied, precision=lax.Precision.HIGHEST)
    depth_out = (depth1.reshape(blocks, 128) + gained[:, :128]).reshape(tile_y, tile_x)
    mass_out = (mass1.reshape(blocks, 128) + gained[:, 128:]).reshape(tile_y, tile_x)
    return (depth_out, mass_out, phase_out, conc_out)


def solution(mesh):
    return jax.shard_map(
        body,
        mesh=mesh,
        in_specs=(
            P("row", "col"),
            P("row", "col"),
            P("row", "col"),
            P("row", "col"),
            P("row", "col"),
            P("row", "col"),
            P(("row", "col")),
            P(("row", "col"), None),
            P(("row", "col")),
            P(("row", "col")),
            P(("row", "col"), None),
            P(("row", "col"), None),
            P(("row", "col"), None),
        ),
        out_specs=(
            P("row", "col"),
            P("row", "col"),
            P(("row", "col"), None),
            P(("row", "col"), None),
        ),
        check_vma=False,
    )
```

```python
import jax
import jax.numpy as jnp
from jax import lax
from jax.experimental import pallas as pl
from jax.experimental.pallas import tpu as pltpu
from jax.sharding import PartitionSpec as P


def halo(fields, axis, dim):
    count = lax.axis_size(axis)
    forward = [(i, i + 1) for i in range(count - 1)]
    backward = [(target, source) for source, target in forward]
    size = fields.shape[dim]
    low = lax.ppermute(lax.index_in_dim(fields, size - 1, axis=dim, keepdims=False), axis, forward)
    high = lax.ppermute(lax.index_in_dim(fields, 0, axis=dim, keepdims=False), axis, backward)
    return low, high


def stencil_kernel(depth_ref, bed_ref, mass_ref, cond_ref, settle_ref, wet_ref, rows_ref, cols_ref,
                   depth1_ref, mass1_ref, surf1_ref):
    depth = depth_ref[...]
    bed = bed_ref[...]
    mass = mass_ref[...]
    cond = cond_ref[...]
    opened = wet_ref[...].astype(jnp.float32)
    surface = depth + bed
    tile_y, tile_x = depth.shape
    own = (surface, mass, cond, opened)
    row_id = lax.broadcasted_iota(jnp.int32, (tile_y, tile_x), 0)
    col_id = lax.broadcasted_iota(jnp.int32, (tile_y, tile_x), 1)
    rows = rows_ref[...]
    cols = cols_ref[...]

    def neighbour(field, step_y, step_x):
        value = own[field]
        if step_y == 1:
            edge = rows[4 + field : 5 + field, :]
            return jnp.where(row_id == tile_y - 1, edge, pltpu.roll(value, tile_y - 1, 0))
        if step_y == -1:
            edge = rows[field : field + 1, :]
            return jnp.where(row_id == 0, edge, pltpu.roll(value, 1, 0))
        if step_x == 1:
            edge = cols[:, 4 + field : 5 + field]
            return jnp.where(col_id == tile_x - 1, edge, pltpu.roll(value, tile_x - 1, 1))
        edge = cols[:, field : field + 1]
        return jnp.where(col_id == 0, edge, pltpu.roll(value, 1, 1))

    water_gain = jnp.zeros_like(depth)
    mass_gain = jnp.zeros_like(depth)
    for step_y, step_x in ((1, 0), (-1, 0), (0, 1), (0, -1)):
        coeff = 0.5 * (cond + neighbour(2, step_y, step_x)) * opened * neighbour(3, step_y, step_x)
        water_gain = water_gain + coeff * (neighbour(0, step_y, step_x) - surface)
        mass_gain = mass_gain + coeff * (neighbour(1, step_y, step_x) - mass)
    depth1 = depth + water_gain
    depth1_ref[...] = depth1
    mass1_ref[...] = (mass + mass_gain) * jnp.exp(-settle_ref[...])
    surf1_ref[...] = depth1 + bed


def smooth_reach(values):
    left = jnp.concatenate([values[:, :1], values[:, :-1]], axis=1)
    right = jnp.concatenate([values[:, 1:], values[:, -1:]], axis=1)
    return values + 0.25 * (left - 2.0 * values + right)


def body(
    depth,
    bed,
    mass,
    conduct,
    settle,
    wet,
    link_block,
    link_owner,
    link_reach,
    link_coef,
    chan_phase,
    chan_conc,
    chan_area,
):
    tile_y, tile_x = depth.shape
    opened = wet.astype(jnp.float32)
    surface = depth + bed
    stacked = jnp.stack([surface, mass, conduct, opened])
    top, bottom = halo(stacked, "row", 1)
    left, right = halo(stacked, "col", 2)
    rows = jnp.concatenate([top, bottom], axis=0)
    cols = jnp.concatenate([left, right], axis=0).T
    tile = jax.ShapeDtypeStruct((tile_y, tile_x), jnp.float32)
    vmem = pl.BlockSpec(memory_space=pltpu.VMEM)
    depth1, mass1, surface1 = pl.pallas_call(
        stencil_kernel,
        out_shape=[tile, tile, tile],
        in_specs=[vmem] * 8,
        out_specs=[vmem] * 3,
        cost_estimate=pl.CostEstimate(
            flops=60 * tile_y * tile_x, transcendentals=tile_y * tile_x, bytes_accessed=36 * tile_y * tile_x
        ),
    )(depth, bed, mass, conduct, settle, wet, rows, cols)

    blocks = tile_y * tile_x // 128
    surf_rows = surface1.reshape(blocks, 128)[link_block]
    mass_rows = mass1.reshape(blocks, 128)[link_block]
    weight = link_coef[:, None] * opened.reshape(blocks, 128)[link_block]
    ws = weight * surf_rows
    wm = weight * mass_rows

    n_row = lax.axis_size("row")
    n_col = lax.axis_size("col")
    devices = n_row * n_col
    links_here = link_owner.shape[0]
    slot_cap = max(2, 2 * links_here // devices)
    target = link_owner[:, 0]
    owner_hot = (target[:, None] == jnp.arange(devices, dtype=jnp.int32)[None, :]).astype(jnp.int32)
    ranking = jnp.sum((jnp.cumsum(owner_hot, axis=0) - 1) * owner_hot, axis=1)
    slot_of = target * slot_cap + ranking
    slot_ids = jnp.arange(devices * slot_cap, dtype=jnp.int32)
    slot_hit = slot_of[None, :] == slot_ids[:, None]
    link_ids = jnp.arange(links_here, dtype=jnp.int32)
    filler = jnp.max(jnp.where(slot_hit, link_ids[None, :], -1), axis=1)
    used = filler >= 0
    source = jnp.maximum(filler, 0)
    payload = jnp.where(used[:, None, None], jnp.stack([ws, wm], axis=1)[source], 0.0)
    tags = jnp.max(jnp.where(slot_hit, link_reach[None, :].astype(jnp.float32), -1.0), axis=1)
    coefs = jnp.maximum(jnp.max(jnp.where(slot_hit, link_coef[None, :], -1.0), axis=1), 0.0)
    meta = jnp.concatenate(
        [tags.reshape(devices, slot_cap), coefs.reshape(devices, slot_cap),
         jnp.zeros((devices, 128 - 2 * slot_cap), jnp.float32)],
        axis=1,
    )
    outgoing = jnp.concatenate([payload.reshape(devices, 2 * slot_cap * 128), meta], axis=1)
    arrived = lax.all_to_all(outgoing, ("row", "col"), split_axis=0, concat_axis=0, tiled=True)
    got = arrived[:, : 2 * slot_cap * 128].reshape(devices * slot_cap, 2, 128)
    arrived_tags = arrived[:, 2 * slot_cap * 128 : 2 * slot_cap * 128 + slot_cap].reshape(devices * slot_cap)
    arrived_coef = arrived[:, 2 * slot_cap * 128 + slot_cap : 2 * slot_cap * 128 + 2 * slot_cap].reshape(
        devices * slot_cap
    )
    got_ws = got[:, 0, :]
    got_wm = got[:, 1, :]
    got_w = jnp.where(got_wm > 0.0, arrived_coef[:, None], 0.0)
    reach_dev = chan_phase.shape[0]
    reach_hot = (arrived_tags[None, :] == jnp.arange(reach_dev, dtype=jnp.float32)[:, None]).astype(
        jnp.float32
    )
    totals = jnp.dot(
        reach_hot, jnp.concatenate([got_ws, got_wm, got_w], axis=1), precision=lax.Precision.HIGHEST
    )
    inflow = totals[:, :128]
    sediment = totals[:, 128:256]
    wet_sum = totals[:, 256:]
    phase_new = (chan_area * chan_phase + inflow) / (chan_area + wet_sum)
    conc_new = (chan_area * chan_conc + sediment) / (chan_area + wet_sum)
    phase_out = smooth_reach(phase_new)
    conc_out = smooth_reach(conc_new)
    reply = jnp.dot(
        reach_hot.T, jnp.concatenate([phase_out, conc_out], axis=1), precision=lax.Precision.HIGHEST
    )
    answered = lax.all_to_all(
        reply.reshape(devices, slot_cap * 256),
        ("row", "col"),
        split_axis=0,
        concat_axis=0,
        tiled=True,
    )
    own_rows = answered.reshape(devices * slot_cap, 256)[slot_of]
    applied = jnp.concatenate(
        [
            0.5 * weight * (own_rows[:, :128] - surf_rows),
            0.5 * weight * (own_rows[:, 128:] - mass_rows),
        ],
        axis=1,
    )
    block_hot = (jnp.arange(blocks, dtype=jnp.int32)[:, None] == link_block[None, :]).astype(
        jnp.float32
    )
    gained = jnp.dot(block_hot, applied, precision=lax.Precision.HIGHEST)
    depth_out = (depth1.reshape(blocks, 128) + gained[:, :128]).reshape(tile_y, tile_x)
    mass_out = (mass1.reshape(blocks, 128) + gained[:, 128:]).reshape(tile_y, tile_x)
    return (depth_out, mass_out, phase_out, conc_out)


def solution(mesh):
    return jax.shard_map(
        body,
        mesh=mesh,
        in_specs=(
            P("row", "col"),
            P("row", "col"),
            P("row", "col"),
            P("row", "col"),
            P("row", "col"),
            P("row", "col"),
            P(("row", "col")),
            P(("row", "col"), None),
            P(("row", "col")),
            P(("row", "col")),
            P(("row", "col"), None),
            P(("row", "col"), None),
            P(("row", "col"), None),
        ),
        out_specs=(
            P("row", "col"),
            P("row", "col"),
            P(("row", "col"), None),
            P(("row", "col"), None),
        ),
        check_vma=False,
    )
```

```python
import jax
import jax.numpy as jnp
from jax import lax
from jax.experimental import pallas as pl
from jax.experimental.pallas import tpu as pltpu
from jax.sharding import PartitionSpec as P


def halo(fields, axis, dim):
    count = lax.axis_size(axis)
    forward = [(i, i + 1) for i in range(count - 1)]
    backward = [(target, source) for source, target in forward]
    size = fields.shape[dim]
    low = lax.ppermute(lax.index_in_dim(fields, size - 1, axis=dim, keepdims=False), axis, forward)
    high = lax.ppermute(lax.index_in_dim(fields, 0, axis=dim, keepdims=False), axis, backward)
    return low, high


def stencil_kernel(depth_ref, bed_ref, mass_ref, cond_ref, settle_ref, wet_ref, rows_ref, cols_ref,
                   depth1_ref, mass1_ref, surf1_ref):
    depth = depth_ref[...]
    bed = bed_ref[...]
    mass = mass_ref[...]
    cond = cond_ref[...]
    opened = wet_ref[...].astype(jnp.float32)
    surface = depth + bed
    tile_y, tile_x = depth.shape
    own = (surface, mass, cond, opened)
    row_id = lax.broadcasted_iota(jnp.int32, (tile_y, tile_x), 0)
    col_id = lax.broadcasted_iota(jnp.int32, (tile_y, tile_x), 1)
    rows = rows_ref[...]
    cols = cols_ref[...]

    def neighbour(field, step_y, step_x):
        value = own[field]
        if step_y == 1:
            edge = rows[4 + field : 5 + field, :]
            return jnp.where(row_id == tile_y - 1, edge, pltpu.roll(value, tile_y - 1, 0))
        if step_y == -1:
            edge = rows[field : field + 1, :]
            return jnp.where(row_id == 0, edge, pltpu.roll(value, 1, 0))
        if step_x == 1:
            edge = cols[:, 4 + field : 5 + field]
            return jnp.where(col_id == tile_x - 1, edge, pltpu.roll(value, tile_x - 1, 1))
        edge = cols[:, field : field + 1]
        return jnp.where(col_id == 0, edge, pltpu.roll(value, 1, 1))

    water_gain = jnp.zeros_like(depth)
    mass_gain = jnp.zeros_like(depth)
    for step_y, step_x in ((1, 0), (-1, 0), (0, 1), (0, -1)):
        coeff = 0.5 * (cond + neighbour(2, step_y, step_x)) * opened * neighbour(3, step_y, step_x)
        water_gain = water_gain + coeff * (neighbour(0, step_y, step_x) - surface)
        mass_gain = mass_gain + coeff * (neighbour(1, step_y, step_x) - mass)
    depth1 = depth + water_gain
    depth1_ref[...] = depth1
    mass1_ref[...] = (mass + mass_gain) * jnp.exp(-settle_ref[...])
    surf1_ref[...] = depth1 + bed


def smooth_reach(values):
    left = jnp.concatenate([values[:, :1], values[:, :-1]], axis=1)
    right = jnp.concatenate([values[:, 1:], values[:, -1:]], axis=1)
    return values + 0.25 * (left - 2.0 * values + right)


def body(
    depth,
    bed,
    mass,
    conduct,
    settle,
    wet,
    link_block,
    link_owner,
    link_reach,
    link_coef,
    chan_phase,
    chan_conc,
    chan_area,
):
    tile_y, tile_x = depth.shape
    opened = wet.astype(jnp.float32)
    surface = depth + bed
    stacked = jnp.stack([surface, mass, conduct, opened])
    top, bottom = halo(stacked, "row", 1)
    left, right = halo(stacked, "col", 2)
    rows = jnp.concatenate([top, bottom], axis=0)
    cols = jnp.concatenate([left, right], axis=0).T
    tile = jax.ShapeDtypeStruct((tile_y, tile_x), jnp.float32)
    vmem = pl.BlockSpec(memory_space=pltpu.VMEM)
    depth1, mass1, surface1 = pl.pallas_call(
        stencil_kernel,
        out_shape=[tile, tile, tile],
        in_specs=[vmem] * 8,
        out_specs=[vmem] * 3,
        cost_estimate=pl.CostEstimate(
            flops=60 * tile_y * tile_x, transcendentals=tile_y * tile_x, bytes_accessed=36 * tile_y * tile_x
        ),
    )(depth, bed, mass, conduct, settle, wet, rows, cols)

    blocks = tile_y * tile_x // 128
    surf_rows = surface1.reshape(blocks, 128)[link_block]
    mass_rows = mass1.reshape(blocks, 128)[link_block]
    weight = link_coef[:, None] * opened.reshape(blocks, 128)[link_block]
    ws = weight * surf_rows
    wm = weight * mass_rows

    n_row = lax.axis_size("row")
    n_col = lax.axis_size("col")
    devices = n_row * n_col
    links_here = link_owner.shape[0]
    slot_cap = max(2, 2 * links_here // devices)
    target = link_owner[:, 0]
    owner_hot = (target[:, None] == jnp.arange(devices, dtype=jnp.int32)[None, :]).astype(jnp.int32)
    ranking = jnp.sum((jnp.cumsum(owner_hot, axis=0) - 1) * owner_hot, axis=1)
    slot_of = target * slot_cap + ranking
    slot_ids = jnp.arange(devices * slot_cap, dtype=jnp.int32)
    slot_hit = slot_of[None, :] == slot_ids[:, None]
    hit = slot_hit.astype(jnp.float32)
    payload = jnp.dot(hit, jnp.concatenate([ws, wm], axis=1), precision=lax.Precision.HIGHEST)
    tags = jnp.max(jnp.where(slot_hit, link_reach[None, :].astype(jnp.float32), -1.0), axis=1)
    coefs = jnp.maximum(jnp.max(jnp.where(slot_hit, link_coef[None, :], -1.0), axis=1), 0.0)
    meta = jnp.concatenate(
        [tags.reshape(devices, slot_cap), coefs.reshape(devices, slot_cap),
         jnp.zeros((devices, 128 - 2 * slot_cap), jnp.float32)],
        axis=1,
    )
    outgoing = jnp.concatenate([payload.reshape(devices, 2 * slot_cap * 128), meta], axis=1)
    arrived = lax.all_to_all(outgoing, ("row", "col"), split_axis=0, concat_axis=0, tiled=True)
    got = arrived[:, : 2 * slot_cap * 128].reshape(devices * slot_cap, 256)
    arrived_tags = arrived[:, 2 * slot_cap * 128 : 2 * slot_cap * 128 + slot_cap].reshape(devices * slot_cap)
    arrived_coef = arrived[:, 2 * slot_cap * 128 + slot_cap : 2 * slot_cap * 128 + 2 * slot_cap].reshape(
        devices * slot_cap
    )
    got_ws = got[:, :128]
    got_wm = got[:, 128:]
    got_w = jnp.where(got_wm > 0.0, arrived_coef[:, None], 0.0)
    reach_dev = chan_phase.shape[0]
    reach_hot = (arrived_tags[None, :] == jnp.arange(reach_dev, dtype=jnp.float32)[:, None]).astype(
        jnp.float32
    )
    totals = jnp.dot(
        reach_hot, jnp.concatenate([got_ws, got_wm, got_w], axis=1), precision=lax.Precision.HIGHEST
    )
    inflow = totals[:, :128]
    sediment = totals[:, 128:256]
    wet_sum = totals[:, 256:]
    phase_new = (chan_area * chan_phase + inflow) / (chan_area + wet_sum)
    conc_new = (chan_area * chan_conc + sediment) / (chan_area + wet_sum)
    phase_out = smooth_reach(phase_new)
    conc_out = smooth_reach(conc_new)
    reply = jnp.dot(
        reach_hot.T, jnp.concatenate([phase_out, conc_out], axis=1), precision=lax.Precision.HIGHEST
    )
    answered = lax.all_to_all(
        reply.reshape(devices, slot_cap * 256),
        ("row", "col"),
        split_axis=0,
        concat_axis=0,
        tiled=True,
    )
    own_rows = answered.reshape(devices * slot_cap, 256)[slot_of]
    applied = jnp.concatenate(
        [
            0.5 * weight * (own_rows[:, :128] - surf_rows),
            0.5 * weight * (own_rows[:, 128:] - mass_rows),
        ],
        axis=1,
    )
    block_hot = (jnp.arange(blocks, dtype=jnp.int32)[:, None] == link_block[None, :]).astype(
        jnp.float32
    )
    gained = jnp.dot(block_hot, applied, precision=lax.Precision.HIGHEST)
    depth_out = (depth1.reshape(blocks, 128) + gained[:, :128]).reshape(tile_y, tile_x)
    mass_out = (mass1.reshape(blocks, 128) + gained[:, 128:]).reshape(tile_y, tile_x)
    return (depth_out, mass_out, phase_out, conc_out)


def solution(mesh):
    return jax.shard_map(
        body,
        mesh=mesh,
        in_specs=(
            P("row", "col"),
            P("row", "col"),
            P("row", "col"),
            P("row", "col"),
            P("row", "col"),
            P("row", "col"),
            P(("row", "col")),
            P(("row", "col"), None),
            P(("row", "col")),
            P(("row", "col")),
            P(("row", "col"), None),
            P(("row", "col"), None),
            P(("row", "col"), None),
        ),
        out_specs=(
            P("row", "col"),
            P("row", "col"),
            P(("row", "col"), None),
            P(("row", "col"), None),
        ),
        check_vma=False,
    )
```

```python
import jax
import jax.numpy as jnp
from jax import lax
from jax.experimental import pallas as pl
from jax.experimental.pallas import tpu as pltpu
from jax.sharding import PartitionSpec as P


def halo_pair(last, first, axis):
    count = lax.axis_size(axis)
    forward = [(i, i + 1) for i in range(count - 1)]
    backward = [(target, source) for source, target in forward]
    return lax.ppermute(last, axis, forward), lax.ppermute(first, axis, backward)


def stencil_kernel(depth_ref, bed_ref, mass_ref, cond_ref, settle_ref, wet_ref, rows_ref, cols_ref,
                   depth1_ref, mass1_ref, surf1_ref):
    depth = depth_ref[...]
    bed = bed_ref[...]
    mass = mass_ref[...]
    cond = cond_ref[...]
    opened = wet_ref[...].astype(jnp.float32)
    surface = depth + bed
    tile_y, tile_x = depth.shape
    own = (surface, mass, cond, opened)
    row_id = lax.broadcasted_iota(jnp.int32, (tile_y, tile_x), 0)
    col_id = lax.broadcasted_iota(jnp.int32, (tile_y, tile_x), 1)
    rows = rows_ref[...]
    cols = cols_ref[...]

    def neighbour(field, step_y, step_x):
        value = own[field]
        if step_y == 1:
            edge = rows[4 + field : 5 + field, :]
            return jnp.where(row_id == tile_y - 1, edge, pltpu.roll(value, tile_y - 1, 0))
        if step_y == -1:
            edge = rows[field : field + 1, :]
            return jnp.where(row_id == 0, edge, pltpu.roll(value, 1, 0))
        if step_x == 1:
            edge = cols[:, 4 + field : 5 + field]
            return jnp.where(col_id == tile_x - 1, edge, pltpu.roll(value, tile_x - 1, 1))
        edge = cols[:, field : field + 1]
        return jnp.where(col_id == 0, edge, pltpu.roll(value, 1, 1))

    water_gain = jnp.zeros_like(depth)
    mass_gain = jnp.zeros_like(depth)
    for step_y, step_x in ((1, 0), (-1, 0), (0, 1), (0, -1)):
        coeff = 0.5 * (cond + neighbour(2, step_y, step_x)) * opened * neighbour(3, step_y, step_x)
        water_gain = water_gain + coeff * (neighbour(0, step_y, step_x) - surface)
        mass_gain = mass_gain + coeff * (neighbour(1, step_y, step_x) - mass)
    depth1 = depth + water_gain
    depth1_ref[...] = depth1
    mass1_ref[...] = (mass + mass_gain) * jnp.exp(-settle_ref[...])
    surf1_ref[...] = depth1 + bed


def smooth_reach(values):
    left = jnp.concatenate([values[:, :1], values[:, :-1]], axis=1)
    right = jnp.concatenate([values[:, 1:], values[:, -1:]], axis=1)
    return values + 0.25 * (left - 2.0 * values + right)


def body(
    depth,
    bed,
    mass,
    conduct,
    settle,
    wet,
    link_block,
    link_owner,
    link_reach,
    link_coef,
    chan_phase,
    chan_conc,
    chan_area,
):
    tile_y, tile_x = depth.shape
    opened = wet.astype(jnp.float32)

    def edges(index, dim):
        def cut(a):
            return lax.index_in_dim(a, index, axis=dim, keepdims=False)
        return jnp.stack([cut(depth) + cut(bed), cut(mass), cut(conduct), cut(wet).astype(jnp.float32)])

    top, bottom = halo_pair(edges(tile_y - 1, 0), edges(0, 0), "row")
    left, right = halo_pair(edges(tile_x - 1, 1), edges(0, 1), "col")
    rows = jnp.concatenate([top, bottom], axis=0)
    cols = jnp.concatenate([left, right], axis=0).T
    tile = jax.ShapeDtypeStruct((tile_y, tile_x), jnp.float32)
    vmem = pl.BlockSpec(memory_space=pltpu.VMEM)
    depth1, mass1, surface1 = pl.pallas_call(
        stencil_kernel,
        out_shape=[tile, tile, tile],
        in_specs=[vmem] * 8,
        out_specs=[vmem] * 3,
        cost_estimate=pl.CostEstimate(
            flops=60 * tile_y * tile_x, transcendentals=tile_y * tile_x, bytes_accessed=36 * tile_y * tile_x
        ),
    )(depth, bed, mass, conduct, settle, wet, rows, cols)

    blocks = tile_y * tile_x // 128
    surf_rows = surface1.reshape(blocks, 128)[link_block]
    mass_rows = mass1.reshape(blocks, 128)[link_block]
    weight = link_coef[:, None] * opened.reshape(blocks, 128)[link_block]
    ws = weight * surf_rows
    wm = weight * mass_rows

    n_row = lax.axis_size("row")
    n_col = lax.axis_size("col")
    devices = n_row * n_col
    links_here = link_owner.shape[0]
    slot_cap = max(2, 2 * links_here // devices)
    target = link_owner[:, 0]
    owner_hot = (target[:, None] == jnp.arange(devices, dtype=jnp.int32)[None, :]).astype(jnp.int32)
    ranking = jnp.sum((jnp.cumsum(owner_hot, axis=0) - 1) * owner_hot, axis=1)
    slot_of = target * slot_cap + ranking
    slot_ids = jnp.arange(devices * slot_cap, dtype=jnp.int32)
    slot_hit = slot_of[None, :] == slot_ids[:, None]
    hit = slot_hit.astype(jnp.float32)
    payload = jnp.dot(hit, jnp.concatenate([ws, wm], axis=1), precision=lax.Precision.HIGHEST)
    tags = jnp.max(jnp.where(slot_hit, link_reach[None, :].astype(jnp.float32), -1.0), axis=1)
    coefs = jnp.maximum(jnp.max(jnp.where(slot_hit, link_coef[None, :], -1.0), axis=1), 0.0)
    meta = jnp.concatenate(
        [tags.reshape(devices, slot_cap), coefs.reshape(devices, slot_cap),
         jnp.zeros((devices, 128 - 2 * slot_cap), jnp.float32)],
        axis=1,
    )
    outgoing = jnp.concatenate([payload.reshape(devices, 2 * slot_cap * 128), meta], axis=1)
    arrived = lax.all_to_all(outgoing, ("row", "col"), split_axis=0, concat_axis=0, tiled=True)
    got = arrived[:, : 2 * slot_cap * 128].reshape(devices * slot_cap, 256)
    arrived_tags = arrived[:, 2 * slot_cap * 128 : 2 * slot_cap * 128 + slot_cap].reshape(devices * slot_cap)
    arrived_coef = arrived[:, 2 * slot_cap * 128 + slot_cap : 2 * slot_cap * 128 + 2 * slot_cap].reshape(
        devices * slot_cap
    )
    got_ws = got[:, :128]
    got_wm = got[:, 128:]
    got_w = jnp.where(got_wm > 0.0, arrived_coef[:, None], 0.0)
    reach_dev = chan_phase.shape[0]
    reach_hot = (arrived_tags[None, :] == jnp.arange(reach_dev, dtype=jnp.float32)[:, None]).astype(
        jnp.float32
    )
    totals = jnp.dot(
        reach_hot, jnp.concatenate([got_ws, got_wm, got_w], axis=1), precision=lax.Precision.HIGHEST
    )
    inflow = totals[:, :128]
    sediment = totals[:, 128:256]
    wet_sum = totals[:, 256:]
    phase_new = (chan_area * chan_phase + inflow) / (chan_area + wet_sum)
    conc_new = (chan_area * chan_conc + sediment) / (chan_area + wet_sum)
    phase_out = smooth_reach(phase_new)
    conc_out = smooth_reach(conc_new)
    reply = jnp.dot(
        reach_hot.T, jnp.concatenate([phase_out, conc_out], axis=1), precision=lax.Precision.HIGHEST
    )
    answered = lax.all_to_all(
        reply.reshape(devices, slot_cap, 256),
        ("row", "col"),
        split_axis=0,
        concat_axis=0,
        tiled=True,
    )
    own_rows = answered.reshape(devices * slot_cap, 256)[slot_of]
    applied = jnp.concatenate(
        [
            0.5 * weight * (own_rows[:, :128] - surf_rows),
            0.5 * weight * (own_rows[:, 128:] - mass_rows),
        ],
        axis=1,
    )
    block_hot = (jnp.arange(blocks, dtype=jnp.int32)[:, None] == link_block[None, :]).astype(
        jnp.float32
    )
    gained = jnp.dot(block_hot, applied, precision=lax.Precision.HIGHEST)
    depth_out = (depth1.reshape(blocks, 128) + gained[:, :128]).reshape(tile_y, tile_x)
    mass_out = (mass1.reshape(blocks, 128) + gained[:, 128:]).reshape(tile_y, tile_x)
    return (depth_out, mass_out, phase_out, conc_out)


def solution(mesh):
    return jax.shard_map(
        body,
        mesh=mesh,
        in_specs=(
            P("row", "col"),
            P("row", "col"),
            P("row", "col"),
            P("row", "col"),
            P("row", "col"),
            P("row", "col"),
            P(("row", "col")),
            P(("row", "col"), None),
            P(("row", "col")),
            P(("row", "col")),
            P(("row", "col"), None),
            P(("row", "col"), None),
            P(("row", "col"), None),
        ),
        out_specs=(
            P("row", "col"),
            P("row", "col"),
            P(("row", "col"), None),
            P(("row", "col"), None),
        ),
        check_vma=False,
    )
```

```python
import jax
import jax.numpy as jnp
from jax import lax
from jax.experimental import pallas as pl
from jax.experimental.pallas import tpu as pltpu
from jax.sharding import PartitionSpec as P


def halo_pair(last, first, axis):
    count = lax.axis_size(axis)
    forward = [(i, i + 1) for i in range(count - 1)]
    backward = [(target, source) for source, target in forward]
    return lax.ppermute(last, axis, forward), lax.ppermute(first, axis, backward)


def stencil_kernel(depth_ref, bed_ref, mass_ref, cond_ref, settle_ref, wet_ref, rows_ref, cols_ref,
                   depth1_ref, mass1_ref, surf1_ref):
    depth = depth_ref[...]
    bed = bed_ref[...]
    mass = mass_ref[...]
    cond = cond_ref[...]
    opened = wet_ref[...].astype(jnp.float32)
    surface = depth + bed
    tile_y, tile_x = depth.shape
    own = (surface, mass, cond, opened)
    row_id = lax.broadcasted_iota(jnp.int32, (tile_y, tile_x), 0)
    col_id = lax.broadcasted_iota(jnp.int32, (tile_y, tile_x), 1)
    rows = rows_ref[...]
    cols = cols_ref[...]

    def neighbour(field, step_y, step_x):
        value = own[field]
        if step_y == 1:
            edge = rows[4 + field : 5 + field, :]
            return jnp.where(row_id == tile_y - 1, edge, pltpu.roll(value, tile_y - 1, 0))
        if step_y == -1:
            edge = rows[field : field + 1, :]
            return jnp.where(row_id == 0, edge, pltpu.roll(value, 1, 0))
        if step_x == 1:
            edge = cols[:, 4 + field : 5 + field]
            return jnp.where(col_id == tile_x - 1, edge, pltpu.roll(value, tile_x - 1, 1))
        edge = cols[:, field : field + 1]
        return jnp.where(col_id == 0, edge, pltpu.roll(value, 1, 1))

    water_gain = jnp.zeros_like(depth)
    mass_gain = jnp.zeros_like(depth)
    for step_y, step_x in ((1, 0), (-1, 0), (0, 1), (0, -1)):
        coeff = 0.5 * (cond + neighbour(2, step_y, step_x)) * opened * neighbour(3, step_y, step_x)
        water_gain = water_gain + coeff * (neighbour(0, step_y, step_x) - surface)
        mass_gain = mass_gain + coeff * (neighbour(1, step_y, step_x) - mass)
    depth1 = depth + water_gain
    depth1_ref[...] = depth1
    mass1_ref[...] = (mass + mass_gain) * jnp.exp(-settle_ref[...])
    surf1_ref[...] = depth1 + bed


def smooth_reach(values):
    left = jnp.concatenate([values[:, :1], values[:, :-1]], axis=1)
    right = jnp.concatenate([values[:, 1:], values[:, -1:]], axis=1)
    return values + 0.25 * (left - 2.0 * values + right)


def body(
    depth,
    bed,
    mass,
    conduct,
    settle,
    wet,
    link_block,
    link_owner,
    link_reach,
    link_coef,
    chan_phase,
    chan_conc,
    chan_area,
):
    tile_y, tile_x = depth.shape
    opened = wet.astype(jnp.float32)

    stacked = jnp.stack([depth + bed, mass, conduct, opened])
    top, bottom = halo_pair(stacked[:, tile_y - 1, :], stacked[:, 0, :], "row")
    left, right = halo_pair(stacked[:, :, tile_x - 1], stacked[:, :, 0], "col")
    rows = jnp.concatenate([top, bottom], axis=0)
    cols = jnp.concatenate([left, right], axis=0).T
    tile = jax.ShapeDtypeStruct((tile_y, tile_x), jnp.float32)
    vmem = pl.BlockSpec(memory_space=pltpu.VMEM)
    depth1, mass1, surface1 = pl.pallas_call(
        stencil_kernel,
        out_shape=[tile, tile, tile],
        in_specs=[vmem] * 8,
        out_specs=[vmem] * 3,
        cost_estimate=pl.CostEstimate(
            flops=60 * tile_y * tile_x, transcendentals=tile_y * tile_x, bytes_accessed=36 * tile_y * tile_x
        ),
    )(depth, bed, mass, conduct, settle, wet, rows, cols)

    blocks = tile_y * tile_x // 128
    surf_rows = surface1.reshape(blocks, 128)[link_block]
    mass_rows = mass1.reshape(blocks, 128)[link_block]
    weight = link_coef[:, None] * opened.reshape(blocks, 128)[link_block]
    ws = weight * surf_rows
    wm = weight * mass_rows

    n_row = lax.axis_size("row")
    n_col = lax.axis_size("col")
    devices = n_row * n_col
    links_here = link_owner.shape[0]
    slot_cap = max(2, 2 * links_here // devices)
    target = link_owner[:, 0]
    owner_hot = (target[:, None] == jnp.arange(devices, dtype=jnp.int32)[None, :]).astype(jnp.int32)
    ranking = jnp.sum((jnp.cumsum(owner_hot, axis=0) - 1) * owner_hot, axis=1)
    slot_of = target * slot_cap + ranking
    slot_ids = jnp.arange(devices * slot_cap, dtype=jnp.int32)
    slot_hit = slot_of[None, :] == slot_ids[:, None]
    hit = slot_hit.astype(jnp.float32)
    payload = jnp.dot(hit, jnp.concatenate([ws, wm], axis=1), precision=lax.Precision.HIGHEST)
    tags = jnp.max(jnp.where(slot_hit, link_reach[None, :].astype(jnp.float32), -1.0), axis=1)
    coefs = jnp.maximum(jnp.max(jnp.where(slot_hit, link_coef[None, :], -1.0), axis=1), 0.0)
    meta = jnp.concatenate(
        [tags.reshape(devices, slot_cap), coefs.reshape(devices, slot_cap),
         jnp.zeros((devices, 128 - 2 * slot_cap), jnp.float32)],
        axis=1,
    )
    outgoing = jnp.concatenate([payload.reshape(devices, 2 * slot_cap * 128), meta], axis=1)
    arrived = lax.all_to_all(outgoing, ("row", "col"), split_axis=0, concat_axis=0, tiled=True)
    got = arrived[:, : 2 * slot_cap * 128].reshape(devices * slot_cap, 256)
    arrived_tags = arrived[:, 2 * slot_cap * 128 : 2 * slot_cap * 128 + slot_cap].reshape(devices * slot_cap)
    arrived_coef = arrived[:, 2 * slot_cap * 128 + slot_cap : 2 * slot_cap * 128 + 2 * slot_cap].reshape(
        devices * slot_cap
    )
    got_ws = got[:, :128]
    got_wm = got[:, 128:]
    got_w = jnp.where(got_wm > 0.0, arrived_coef[:, None], 0.0)
    reach_dev = chan_phase.shape[0]
    reach_hot = (arrived_tags[None, :] == jnp.arange(reach_dev, dtype=jnp.float32)[:, None]).astype(
        jnp.float32
    )
    totals = jnp.dot(
        reach_hot, jnp.concatenate([got_ws, got_wm, got_w], axis=1), precision=lax.Precision.HIGHEST
    )
    inflow = totals[:, :128]
    sediment = totals[:, 128:256]
    wet_sum = totals[:, 256:]
    phase_new = (chan_area * chan_phase + inflow) / (chan_area + wet_sum)
    conc_new = (chan_area * chan_conc + sediment) / (chan_area + wet_sum)
    phase_out = smooth_reach(phase_new)
    conc_out = smooth_reach(conc_new)
    reply = jnp.dot(
        reach_hot.T, jnp.concatenate([phase_out, conc_out], axis=1), precision=lax.Precision.HIGHEST
    )
    answered = lax.all_to_all(
        reply.reshape(devices, slot_cap, 256),
        ("row", "col"),
        split_axis=0,
        concat_axis=0,
        tiled=True,
    )
    own_rows = answered.reshape(devices * slot_cap, 256)[slot_of]
    applied = jnp.concatenate(
        [
            0.5 * weight * (own_rows[:, :128] - surf_rows),
            0.5 * weight * (own_rows[:, 128:] - mass_rows),
        ],
        axis=1,
    )
    block_hot = (jnp.arange(blocks, dtype=jnp.int32)[:, None] == link_block[None, :]).astype(
        jnp.float32
    )
    gained = jnp.dot(block_hot, applied, precision=lax.Precision.HIGHEST)
    depth_out = (depth1.reshape(blocks, 128) + gained[:, :128]).reshape(tile_y, tile_x)
    mass_out = (mass1.reshape(blocks, 128) + gained[:, 128:]).reshape(tile_y, tile_x)
    return (depth_out, mass_out, phase_out, conc_out)


def solution(mesh):
    return jax.shard_map(
        body,
        mesh=mesh,
        in_specs=(
            P("row", "col"),
            P("row", "col"),
            P("row", "col"),
            P("row", "col"),
            P("row", "col"),
            P("row", "col"),
            P(("row", "col")),
            P(("row", "col"), None),
            P(("row", "col")),
            P(("row", "col")),
            P(("row", "col"), None),
            P(("row", "col"), None),
            P(("row", "col"), None),
        ),
        out_specs=(
            P("row", "col"),
            P("row", "col"),
            P(("row", "col"), None),
            P(("row", "col"), None),
        ),
        check_vma=False,
    )
```

```python
import jax
import jax.numpy as jnp
from jax import lax
from jax.experimental import pallas as pl
from jax.experimental.pallas import tpu as pltpu
from jax.sharding import PartitionSpec as P


def halo_pair(last, first, axis):
    count = lax.axis_size(axis)
    forward = [(i, i + 1) for i in range(count - 1)]
    backward = [(target, source) for source, target in forward]
    return lax.ppermute(last, axis, forward), lax.ppermute(first, axis, backward)


def stencil_kernel(depth_ref, bed_ref, mass_ref, cond_ref, settle_ref, wet_ref, rows_ref, cols_ref,
                   depth1_ref, mass1_ref, surf_blocks_ref, mass_blocks_ref, open_blocks_ref):
    depth = depth_ref[...]
    bed = bed_ref[...]
    mass = mass_ref[...]
    cond = cond_ref[...]
    opened = wet_ref[...].astype(jnp.float32)
    surface = depth + bed
    tile_y, tile_x = depth.shape
    own = (surface, mass, cond, opened)
    row_id = lax.broadcasted_iota(jnp.int32, (tile_y, tile_x), 0)
    col_id = lax.broadcasted_iota(jnp.int32, (tile_y, tile_x), 1)
    rows = rows_ref[...]
    cols = cols_ref[...]

    def neighbour(field, step_y, step_x):
        value = own[field]
        if step_y == 1:
            edge = rows[4 + field : 5 + field, :]
            return jnp.where(row_id == tile_y - 1, edge, pltpu.roll(value, tile_y - 1, 0))
        if step_y == -1:
            edge = rows[field : field + 1, :]
            return jnp.where(row_id == 0, edge, pltpu.roll(value, 1, 0))
        if step_x == 1:
            edge = cols[:, 4 + field : 5 + field]
            return jnp.where(col_id == tile_x - 1, edge, pltpu.roll(value, tile_x - 1, 1))
        edge = cols[:, field : field + 1]
        return jnp.where(col_id == 0, edge, pltpu.roll(value, 1, 1))

    water_gain = jnp.zeros_like(depth)
    mass_gain = jnp.zeros_like(depth)
    for step_y, step_x in ((1, 0), (-1, 0), (0, 1), (0, -1)):
        coeff = 0.5 * (cond + neighbour(2, step_y, step_x)) * opened * neighbour(3, step_y, step_x)
        water_gain = water_gain + coeff * (neighbour(0, step_y, step_x) - surface)
        mass_gain = mass_gain + coeff * (neighbour(1, step_y, step_x) - mass)
    depth1 = depth + water_gain
    mass1 = (mass + mass_gain) * jnp.exp(-settle_ref[...])
    depth1_ref[...] = depth1
    mass1_ref[...] = mass1
    per_row = tile_x // 128
    for j in range(per_row):
        lanes = slice(j * 128, (j + 1) * 128)
        rows_j = pl.ds(j, tile_y, stride=per_row)
        surf_blocks_ref[rows_j, :] = (depth1 + bed)[:, lanes]
        mass_blocks_ref[rows_j, :] = mass1[:, lanes]
        open_blocks_ref[rows_j, :] = opened[:, lanes]


def smooth_reach(values):
    left = jnp.concatenate([values[:, :1], values[:, :-1]], axis=1)
    right = jnp.concatenate([values[:, 1:], values[:, -1:]], axis=1)
    return values + 0.25 * (left - 2.0 * values + right)


def body(
    depth,
    bed,
    mass,
    conduct,
    settle,
    wet,
    link_block,
    link_owner,
    link_reach,
    link_coef,
    chan_phase,
    chan_conc,
    chan_area,
):
    tile_y, tile_x = depth.shape
    opened = wet.astype(jnp.float32)

    stacked = jnp.stack([depth + bed, mass, conduct, opened])
    top, bottom = halo_pair(stacked[:, tile_y - 1, :], stacked[:, 0, :], "row")
    left, right = halo_pair(stacked[:, :, tile_x - 1], stacked[:, :, 0], "col")
    rows = jnp.concatenate([top, bottom], axis=0)
    cols = jnp.concatenate([left, right], axis=0).T
    tile = jax.ShapeDtypeStruct((tile_y, tile_x), jnp.float32)
    vmem = pl.BlockSpec(memory_space=pltpu.VMEM)
    blocks = tile_y * tile_x // 128
    block_rows = jax.ShapeDtypeStruct((blocks, 128), jnp.float32)
    depth1, mass1, surf_blocks, mass_blocks, open_blocks = pl.pallas_call(
        stencil_kernel,
        out_shape=[tile, tile, block_rows, block_rows, block_rows],
        in_specs=[vmem] * 8,
        out_specs=[vmem] * 5,
        cost_estimate=pl.CostEstimate(
            flops=60 * tile_y * tile_x, transcendentals=tile_y * tile_x, bytes_accessed=44 * tile_y * tile_x
        ),
    )(depth, bed, mass, conduct, settle, wet, rows, cols)

    surf_rows = surf_blocks[link_block]
    mass_rows = mass_blocks[link_block]
    weight = link_coef[:, None] * open_blocks[link_block]
    ws = weight * surf_rows
    wm = weight * mass_rows

    n_row = lax.axis_size("row")
    n_col = lax.axis_size("col")
    devices = n_row * n_col
    links_here = link_owner.shape[0]
    slot_cap = max(2, 2 * links_here // devices)
    target = link_owner[:, 0]
    owner_hot = (target[:, None] == jnp.arange(devices, dtype=jnp.int32)[None, :]).astype(jnp.int32)
    ranking = jnp.sum((jnp.cumsum(owner_hot, axis=0) - 1) * owner_hot, axis=1)
    slot_of = target * slot_cap + ranking
    slot_ids = jnp.arange(devices * slot_cap, dtype=jnp.int32)
    slot_hit = slot_of[None, :] == slot_ids[:, None]
    hit = slot_hit.astype(jnp.float32)
    payload = jnp.dot(hit, jnp.concatenate([ws, wm], axis=1), precision=lax.Precision.HIGHEST)
    tags = jnp.max(jnp.where(slot_hit, link_reach[None, :].astype(jnp.float32), -1.0), axis=1)
    coefs = jnp.maximum(jnp.max(jnp.where(slot_hit, link_coef[None, :], -1.0), axis=1), 0.0)
    meta = jnp.concatenate(
        [tags.reshape(devices, slot_cap), coefs.reshape(devices, slot_cap),
         jnp.zeros((devices, 128 - 2 * slot_cap), jnp.float32)],
        axis=1,
    )
    outgoing = jnp.concatenate([payload.reshape(devices, 2 * slot_cap * 128), meta], axis=1)
    arrived = lax.all_to_all(outgoing, ("row", "col"), split_axis=0, concat_axis=0, tiled=True)
    got = arrived[:, : 2 * slot_cap * 128].reshape(devices * slot_cap, 256)
    arrived_tags = arrived[:, 2 * slot_cap * 128 : 2 * slot_cap * 128 + slot_cap].reshape(devices * slot_cap)
    arrived_coef = arrived[:, 2 * slot_cap * 128 + slot_cap : 2 * slot_cap * 128 + 2 * slot_cap].reshape(
        devices * slot_cap
    )
    got_ws = got[:, :128]
    got_wm = got[:, 128:]
    got_w = jnp.where(got_wm > 0.0, arrived_coef[:, None], 0.0)
    reach_dev = chan_phase.shape[0]
    reach_hot = (arrived_tags[None, :] == jnp.arange(reach_dev, dtype=jnp.float32)[:, None]).astype(
        jnp.float32
    )
    totals = jnp.dot(
        reach_hot, jnp.concatenate([got_ws, got_wm, got_w], axis=1), precision=lax.Precision.HIGHEST
    )
    inflow = totals[:, :128]
    sediment = totals[:, 128:256]
    wet_sum = totals[:, 256:]
    phase_new = (chan_area * chan_phase + inflow) / (chan_area + wet_sum)
    conc_new = (chan_area * chan_conc + sediment) / (chan_area + wet_sum)
    phase_out = smooth_reach(phase_new)
    conc_out = smooth_reach(conc_new)
    reply = jnp.dot(
        reach_hot.T, jnp.concatenate([phase_out, conc_out], axis=1), precision=lax.Precision.HIGHEST
    )
    answered = lax.all_to_all(
        reply.reshape(devices, slot_cap, 256),
        ("row", "col"),
        split_axis=0,
        concat_axis=0,
        tiled=True,
    )
    own_rows = answered.reshape(devices * slot_cap, 256)[slot_of]
    applied = jnp.concatenate(
        [
            0.5 * weight * (own_rows[:, :128] - surf_rows),
            0.5 * weight * (own_rows[:, 128:] - mass_rows),
        ],
        axis=1,
    )
    per_row = tile_x // 128
    row_ids = jnp.arange(tile_y, dtype=jnp.int32)[:, None]
    gained = [
        jnp.dot(
            (row_ids * per_row + j == link_block[None, :]).astype(jnp.float32),
            applied,
            precision=lax.Precision.HIGHEST,
        )
        for j in range(per_row)
    ]
    depth_out = depth1 + jnp.concatenate([g[:, :128] for g in gained], axis=1)
    mass_out = mass1 + jnp.concatenate([g[:, 128:] for g in gained], axis=1)
    return (depth_out, mass_out, phase_out, conc_out)


def solution(mesh):
    return jax.shard_map(
        body,
        mesh=mesh,
        in_specs=(
            P("row", "col"),
            P("row", "col"),
            P("row", "col"),
            P("row", "col"),
            P("row", "col"),
            P("row", "col"),
            P(("row", "col")),
            P(("row", "col"), None),
            P(("row", "col")),
            P(("row", "col")),
            P(("row", "col"), None),
            P(("row", "col"), None),
            P(("row", "col"), None),
        ),
        out_specs=(
            P("row", "col"),
            P("row", "col"),
            P(("row", "col"), None),
            P(("row", "col"), None),
        ),
        check_vma=False,
    )
```

```python
import jax
import jax.numpy as jnp
from jax import lax
from jax.experimental import pallas as pl
from jax.experimental.pallas import tpu as pltpu
from jax.sharding import PartitionSpec as P


def halo_pair(last, first, axis):
    count = lax.axis_size(axis)
    forward = [(i, i + 1) for i in range(count - 1)]
    backward = [(target, source) for source, target in forward]
    return lax.ppermute(last, axis, forward), lax.ppermute(first, axis, backward)


def stencil_kernel(depth_ref, bed_ref, mass_ref, cond_ref, settle_ref, wet_ref, rows_ref, cols_ref,
                   depth1_ref, mass1_ref, surf_blocks_ref, mass_blocks_ref, open_blocks_ref,
                   open_surf_ref, open_mass_ref):
    depth = depth_ref[...]
    bed = bed_ref[...]
    mass = mass_ref[...]
    cond = cond_ref[...]
    opened = wet_ref[...].astype(jnp.float32)
    surface = depth + bed
    tile_y, tile_x = depth.shape
    own = (surface, mass, cond, opened)
    row_id = lax.broadcasted_iota(jnp.int32, (tile_y, tile_x), 0)
    col_id = lax.broadcasted_iota(jnp.int32, (tile_y, tile_x), 1)
    rows = rows_ref[...]
    cols = cols_ref[...]

    def neighbour(field, step_y, step_x):
        value = own[field]
        if step_y == 1:
            edge = rows[4 + field : 5 + field, :]
            return jnp.where(row_id == tile_y - 1, edge, pltpu.roll(value, tile_y - 1, 0))
        if step_y == -1:
            edge = rows[field : field + 1, :]
            return jnp.where(row_id == 0, edge, pltpu.roll(value, 1, 0))
        if step_x == 1:
            edge = cols[:, 4 + field : 5 + field]
            return jnp.where(col_id == tile_x - 1, edge, pltpu.roll(value, tile_x - 1, 1))
        edge = cols[:, field : field + 1]
        return jnp.where(col_id == 0, edge, pltpu.roll(value, 1, 1))

    water_gain = jnp.zeros_like(depth)
    mass_gain = jnp.zeros_like(depth)
    for step_y, step_x in ((1, 0), (-1, 0), (0, 1), (0, -1)):
        coeff = 0.5 * (cond + neighbour(2, step_y, step_x)) * opened * neighbour(3, step_y, step_x)
        water_gain = water_gain + coeff * (neighbour(0, step_y, step_x) - surface)
        mass_gain = mass_gain + coeff * (neighbour(1, step_y, step_x) - mass)
    depth1 = depth + water_gain
    mass1 = (mass + mass_gain) * jnp.exp(-settle_ref[...])
    depth1_ref[...] = depth1
    mass1_ref[...] = mass1
    per_row = tile_x // 128
    for j in range(per_row):
        lanes = slice(j * 128, (j + 1) * 128)
        rows_j = pl.ds(j, tile_y, stride=per_row)
        surf_j = (depth1 + bed)[:, lanes]
        mass_j = mass1[:, lanes]
        open_j = opened[:, lanes]
        surf_blocks_ref[rows_j, :] = surf_j
        mass_blocks_ref[rows_j, :] = mass_j
        open_blocks_ref[rows_j, :] = open_j
        open_surf_ref[rows_j, :] = open_j * surf_j
        open_mass_ref[rows_j, :] = open_j * mass_j


def smooth_reach(values):
    left = jnp.concatenate([values[:, :1], values[:, :-1]], axis=1)
    right = jnp.concatenate([values[:, 1:], values[:, -1:]], axis=1)
    return values + 0.25 * (left - 2.0 * values + right)


def body(
    depth,
    bed,
    mass,
    conduct,
    settle,
    wet,
    link_block,
    link_owner,
    link_reach,
    link_coef,
    chan_phase,
    chan_conc,
    chan_area,
):
    tile_y, tile_x = depth.shape
    opened = wet.astype(jnp.float32)

    stacked = jnp.stack([depth + bed, mass, conduct, opened])
    top, bottom = halo_pair(stacked[:, tile_y - 1, :], stacked[:, 0, :], "row")
    left, right = halo_pair(stacked[:, :, tile_x - 1], stacked[:, :, 0], "col")
    rows = jnp.concatenate([top, bottom], axis=0)
    cols = jnp.concatenate([left, right], axis=0).T
    tile = jax.ShapeDtypeStruct((tile_y, tile_x), jnp.float32)
    vmem = pl.BlockSpec(memory_space=pltpu.VMEM)
    blocks = tile_y * tile_x // 128
    block_rows = jax.ShapeDtypeStruct((blocks, 128), jnp.float32)
    depth1, mass1, surf_blocks, mass_blocks, open_blocks, open_surf, open_mass = pl.pallas_call(
        stencil_kernel,
        out_shape=[tile, tile] + [block_rows] * 5,
        in_specs=[vmem] * 8,
        out_specs=[vmem] * 7,
        cost_estimate=pl.CostEstimate(
            flops=60 * tile_y * tile_x, transcendentals=tile_y * tile_x, bytes_accessed=52 * tile_y * tile_x
        ),
    )(depth, bed, mass, conduct, settle, wet, rows, cols)

    n_row = lax.axis_size("row")
    n_col = lax.axis_size("col")
    devices = n_row * n_col
    links_here = link_owner.shape[0]
    slot_cap = max(2, 2 * links_here // devices)
    target = link_owner[:, 0]
    owner_hot = (target[:, None] == jnp.arange(devices, dtype=jnp.int32)[None, :]).astype(jnp.int32)
    ranking = jnp.sum((jnp.cumsum(owner_hot, axis=0) - 1) * owner_hot, axis=1)
    slot_of = target * slot_cap + ranking
    slot_ids = jnp.arange(devices * slot_cap, dtype=jnp.int32)
    slot_hit = slot_of[None, :] == slot_ids[:, None]
    slot_block = jnp.max(jnp.where(slot_hit, link_block[None, :], -1), axis=1)
    block_ids = jnp.arange(blocks, dtype=jnp.int32)
    slot_hot = (slot_block[:, None] == block_ids[None, :]).astype(jnp.float32)
    coefs = jnp.maximum(jnp.max(jnp.where(slot_hit, link_coef[None, :], -1.0), axis=1), 0.0)
    payload = coefs[:, None] * jnp.dot(
        slot_hot, jnp.concatenate([open_surf, open_mass], axis=1), precision=lax.Precision.HIGHEST
    )
    tags = jnp.max(jnp.where(slot_hit, link_reach[None, :].astype(jnp.float32), -1.0), axis=1)
    meta = jnp.concatenate(
        [tags.reshape(devices, slot_cap), coefs.reshape(devices, slot_cap),
         jnp.zeros((devices, 128 - 2 * slot_cap), jnp.float32)],
        axis=1,
    )
    outgoing = jnp.concatenate([payload.reshape(devices, 2 * slot_cap * 128), meta], axis=1)
    arrived = lax.all_to_all(outgoing, ("row", "col"), split_axis=0, concat_axis=0, tiled=True)
    got = arrived[:, : 2 * slot_cap * 128].reshape(devices * slot_cap, 256)
    arrived_tags = arrived[:, 2 * slot_cap * 128 : 2 * slot_cap * 128 + slot_cap].reshape(devices * slot_cap)
    arrived_coef = arrived[:, 2 * slot_cap * 128 + slot_cap : 2 * slot_cap * 128 + 2 * slot_cap].reshape(
        devices * slot_cap
    )
    got_ws = got[:, :128]
    got_wm = got[:, 128:]
    got_w = jnp.where(got_wm > 0.0, arrived_coef[:, None], 0.0)
    reach_dev = chan_phase.shape[0]
    reach_hot = (arrived_tags[None, :] == jnp.arange(reach_dev, dtype=jnp.float32)[:, None]).astype(
        jnp.float32
    )
    totals = jnp.dot(
        reach_hot, jnp.concatenate([got_ws, got_wm, got_w], axis=1), precision=lax.Precision.HIGHEST
    )
    inflow = totals[:, :128]
    sediment = totals[:, 128:256]
    wet_sum = totals[:, 256:]
    phase_new = (chan_area * chan_phase + inflow) / (chan_area + wet_sum)
    conc_new = (chan_area * chan_conc + sediment) / (chan_area + wet_sum)
    phase_out = smooth_reach(phase_new)
    conc_out = smooth_reach(conc_new)
    reply = jnp.dot(
        reach_hot.T, jnp.concatenate([phase_out, conc_out], axis=1), precision=lax.Precision.HIGHEST
    )
    answered = lax.all_to_all(
        reply.reshape(devices, slot_cap, 256),
        ("row", "col"),
        split_axis=0,
        concat_axis=0,
        tiled=True,
    )
    own_rows = answered.reshape(devices * slot_cap, 256)[slot_of]
    surf_rows = surf_blocks[link_block]
    mass_rows = mass_blocks[link_block]
    weight = link_coef[:, None] * open_blocks[link_block]
    applied = jnp.concatenate(
        [
            0.5 * weight * (own_rows[:, :128] - surf_rows),
            0.5 * weight * (own_rows[:, 128:] - mass_rows),
        ],
        axis=1,
    )
    per_row = tile_x // 128
    row_ids = jnp.arange(tile_y, dtype=jnp.int32)[:, None]
    gained = [
        jnp.dot(
            (row_ids * per_row + j == link_block[None, :]).astype(jnp.float32),
            applied,
            precision=lax.Precision.HIGHEST,
        )
        for j in range(per_row)
    ]
    depth_out = depth1 + jnp.concatenate([g[:, :128] for g in gained], axis=1)
    mass_out = mass1 + jnp.concatenate([g[:, 128:] for g in gained], axis=1)
    return (depth_out, mass_out, phase_out, conc_out)


def solution(mesh):
    return jax.shard_map(
        body,
        mesh=mesh,
        in_specs=(
            P("row", "col"),
            P("row", "col"),
            P("row", "col"),
            P("row", "col"),
            P("row", "col"),
            P("row", "col"),
            P(("row", "col")),
            P(("row", "col"), None),
            P(("row", "col")),
            P(("row", "col")),
            P(("row", "col"), None),
            P(("row", "col"), None),
            P(("row", "col"), None),
        ),
        out_specs=(
            P("row", "col"),
            P("row", "col"),
            P(("row", "col"), None),
            P(("row", "col"), None),
        ),
        check_vma=False,
    )
```

```python
import jax
import jax.numpy as jnp
from jax import lax
from jax.experimental import pallas as pl
from jax.experimental.pallas import tpu as pltpu
from jax.sharding import PartitionSpec as P


def halo_pair(last, first, axis):
    count = lax.axis_size(axis)
    forward = [(i, i + 1) for i in range(count - 1)]
    backward = [(target, source) for source, target in forward]
    return lax.ppermute(last, axis, forward), lax.ppermute(first, axis, backward)


def stencil_kernel(depth_ref, bed_ref, mass_ref, cond_ref, settle_ref, wet_ref, rows_ref, cols_ref,
                   depth1_ref, mass1_ref, surf_blocks_ref, mass_blocks_ref, open_blocks_ref,
                   open_surf_ref, open_mass_ref):
    depth = depth_ref[...]
    bed = bed_ref[...]
    mass = mass_ref[...]
    cond = cond_ref[...]
    opened = wet_ref[...].astype(jnp.float32)
    surface = depth + bed
    tile_y, tile_x = depth.shape
    own = (surface, mass, cond, opened)
    row_id = lax.broadcasted_iota(jnp.int32, (tile_y, tile_x), 0)
    col_id = lax.broadcasted_iota(jnp.int32, (tile_y, tile_x), 1)
    rows = rows_ref[...]
    cols = cols_ref[...]

    def neighbour(field, step_y, step_x):
        value = own[field]
        if step_y == 1:
            edge = rows[4 + field : 5 + field, :]
            return jnp.where(row_id == tile_y - 1, edge, pltpu.roll(value, tile_y - 1, 0))
        if step_y == -1:
            edge = rows[field : field + 1, :]
            return jnp.where(row_id == 0, edge, pltpu.roll(value, 1, 0))
        if step_x == 1:
            edge = cols[:, 4 + field : 5 + field]
            return jnp.where(col_id == tile_x - 1, edge, pltpu.roll(value, tile_x - 1, 1))
        edge = cols[:, field : field + 1]
        return jnp.where(col_id == 0, edge, pltpu.roll(value, 1, 1))

    water_gain = jnp.zeros_like(depth)
    mass_gain = jnp.zeros_like(depth)
    for step_y, step_x in ((1, 0), (-1, 0), (0, 1), (0, -1)):
        coeff = 0.5 * (cond + neighbour(2, step_y, step_x)) * opened * neighbour(3, step_y, step_x)
        water_gain = water_gain + coeff * (neighbour(0, step_y, step_x) - surface)
        mass_gain = mass_gain + coeff * (neighbour(1, step_y, step_x) - mass)
    depth1 = depth + water_gain
    mass1 = (mass + mass_gain) * jnp.exp(-settle_ref[...])
    depth1_ref[...] = depth1
    mass1_ref[...] = mass1
    per_row = tile_x // 128
    for j in range(per_row):
        lanes = slice(j * 128, (j + 1) * 128)
        rows_j = pl.ds(j, tile_y, stride=per_row)
        surf_j = (depth1 + bed)[:, lanes]
        mass_j = mass1[:, lanes]
        open_j = opened[:, lanes]
        surf_blocks_ref[rows_j, :] = surf_j
        mass_blocks_ref[rows_j, :] = mass_j
        open_blocks_ref[rows_j, :] = open_j
        open_surf_ref[rows_j, :] = open_j * surf_j
        open_mass_ref[rows_j, :] = open_j * mass_j


def pick_dot(hot, values):
    def part(x):
        return lax.reduce_precision(x, exponent_bits=8, mantissa_bits=7)

    hi = part(values)
    rest = values - hi
    mid = part(rest)
    lo = rest - mid
    hot = hot.astype(jnp.bfloat16)

    def one(x):
        return jnp.dot(hot, x.astype(jnp.bfloat16), preferred_element_type=jnp.float32)

    return (one(hi) + one(mid)) + one(lo)


def smooth_reach(values):
    left = jnp.concatenate([values[:, :1], values[:, :-1]], axis=1)
    right = jnp.concatenate([values[:, 1:], values[:, -1:]], axis=1)
    return values + 0.25 * (left - 2.0 * values + right)


def body(
    depth,
    bed,
    mass,
    conduct,
    settle,
    wet,
    link_block,
    link_owner,
    link_reach,
    link_coef,
    chan_phase,
    chan_conc,
    chan_area,
):
    tile_y, tile_x = depth.shape
    opened = wet.astype(jnp.float32)

    stacked = jnp.stack([depth + bed, mass, conduct, opened])
    top, bottom = halo_pair(stacked[:, tile_y - 1, :], stacked[:, 0, :], "row")
    left, right = halo_pair(stacked[:, :, tile_x - 1], stacked[:, :, 0], "col")
    rows = jnp.concatenate([top, bottom], axis=0)
    cols = jnp.concatenate([left, right], axis=0).T
    tile = jax.ShapeDtypeStruct((tile_y, tile_x), jnp.float32)
    vmem = pl.BlockSpec(memory_space=pltpu.VMEM)
    blocks = tile_y * tile_x // 128
    block_rows = jax.ShapeDtypeStruct((blocks, 128), jnp.float32)
    depth1, mass1, surf_blocks, mass_blocks, open_blocks, open_surf, open_mass = pl.pallas_call(
        stencil_kernel,
        out_shape=[tile, tile] + [block_rows] * 5,
        in_specs=[vmem] * 8,
        out_specs=[vmem] * 7,
        cost_estimate=pl.CostEstimate(
            flops=60 * tile_y * tile_x, transcendentals=tile_y * tile_x, bytes_accessed=52 * tile_y * tile_x
        ),
    )(depth, bed, mass, conduct, settle, wet, rows, cols)

    n_row = lax.axis_size("row")
    n_col = lax.axis_size("col")
    devices = n_row * n_col
    links_here = link_owner.shape[0]
    slot_cap = max(2, 2 * links_here // devices)
    target = link_owner[:, 0]
    owner_hot = (target[:, None] == jnp.arange(devices, dtype=jnp.int32)[None, :]).astype(jnp.int32)
    ranking = jnp.sum((jnp.cumsum(owner_hot, axis=0) - 1) * owner_hot, axis=1)
    slot_of = target * slot_cap + ranking
    slot_ids = jnp.arange(devices * slot_cap, dtype=jnp.int32)
    slot_hit = slot_of[None, :] == slot_ids[:, None]
    slot_block = jnp.max(jnp.where(slot_hit, link_block[None, :], -1), axis=1)
    block_ids = jnp.arange(blocks, dtype=jnp.int32)
    slot_hot = (slot_block[:, None] == block_ids[None, :]).astype(jnp.float32)
    coefs = jnp.maximum(jnp.max(jnp.where(slot_hit, link_coef[None, :], -1.0), axis=1), 0.0)
    payload = coefs[:, None] * pick_dot(slot_hot, jnp.concatenate([open_surf, open_mass], axis=1))
    tags = jnp.max(jnp.where(slot_hit, link_reach[None, :].astype(jnp.float32), -1.0), axis=1)
    meta = jnp.concatenate(
        [tags.reshape(devices, slot_cap), coefs.reshape(devices, slot_cap),
         jnp.zeros((devices, 128 - 2 * slot_cap), jnp.float32)],
        axis=1,
    )
    outgoing = jnp.concatenate([payload.reshape(devices, 2 * slot_cap * 128), meta], axis=1)
    arrived = lax.all_to_all(outgoing, ("row", "col"), split_axis=0, concat_axis=0, tiled=True)
    got = arrived[:, : 2 * slot_cap * 128].reshape(devices * slot_cap, 256)
    arrived_tags = arrived[:, 2 * slot_cap * 128 : 2 * slot_cap * 128 + slot_cap].reshape(devices * slot_cap)
    arrived_coef = arrived[:, 2 * slot_cap * 128 + slot_cap : 2 * slot_cap * 128 + 2 * slot_cap].reshape(
        devices * slot_cap
    )
    got_ws = got[:, :128]
    got_wm = got[:, 128:]
    got_w = jnp.where(got_wm > 0.0, arrived_coef[:, None], 0.0)
    reach_dev = chan_phase.shape[0]
    reach_hot = (arrived_tags[None, :] == jnp.arange(reach_dev, dtype=jnp.float32)[:, None]).astype(
        jnp.float32
    )
    totals = jnp.dot(
        reach_hot, jnp.concatenate([got_ws, got_wm, got_w], axis=1), precision=lax.Precision.HIGHEST
    )
    inflow = totals[:, :128]
    sediment = totals[:, 128:256]
    wet_sum = totals[:, 256:]
    phase_new = (chan_area * chan_phase + inflow) / (chan_area + wet_sum)
    conc_new = (chan_area * chan_conc + sediment) / (chan_area + wet_sum)
    phase_out = smooth_reach(phase_new)
    conc_out = smooth_reach(conc_new)
    reply = pick_dot(reach_hot.T, jnp.concatenate([phase_out, conc_out], axis=1))
    answered = lax.all_to_all(
        reply.reshape(devices, slot_cap, 256),
        ("row", "col"),
        split_axis=0,
        concat_axis=0,
        tiled=True,
    )
    own_rows = answered.reshape(devices * slot_cap, 256)[slot_of]
    surf_rows = surf_blocks[link_block]
    mass_rows = mass_blocks[link_block]
    weight = link_coef[:, None] * open_blocks[link_block]
    applied = jnp.concatenate(
        [
            0.5 * weight * (own_rows[:, :128] - surf_rows),
            0.5 * weight * (own_rows[:, 128:] - mass_rows),
        ],
        axis=1,
    )
    per_row = tile_x // 128
    row_ids = jnp.arange(tile_y, dtype=jnp.int32)[:, None]
    gained = [
        pick_dot((row_ids * per_row + j == link_block[None, :]).astype(jnp.float32), applied)
        for j in range(per_row)
    ]
    depth_out = depth1 + jnp.concatenate([g[:, :128] for g in gained], axis=1)
    mass_out = mass1 + jnp.concatenate([g[:, 128:] for g in gained], axis=1)
    return (depth_out, mass_out, phase_out, conc_out)


def solution(mesh):
    return jax.shard_map(
        body,
        mesh=mesh,
        in_specs=(
            P("row", "col"),
            P("row", "col"),
            P("row", "col"),
            P("row", "col"),
            P("row", "col"),
            P("row", "col"),
            P(("row", "col")),
            P(("row", "col"), None),
            P(("row", "col")),
            P(("row", "col")),
            P(("row", "col"), None),
            P(("row", "col"), None),
            P(("row", "col"), None),
        ),
        out_specs=(
            P("row", "col"),
            P("row", "col"),
            P(("row", "col"), None),
            P(("row", "col"), None),
        ),
        check_vma=False,
    )
```

```python
import jax
import jax.numpy as jnp
from jax import lax
from jax.experimental import pallas as pl
from jax.experimental.pallas import tpu as pltpu
from jax.sharding import PartitionSpec as P


def halo_pair(last, first, axis):
    count = lax.axis_size(axis)
    forward = [(i, i + 1) for i in range(count - 1)]
    backward = [(target, source) for source, target in forward]
    return lax.ppermute(last, axis, forward), lax.ppermute(first, axis, backward)


def stencil_kernel(depth_ref, bed_ref, mass_ref, cond_ref, settle_ref, wet_ref, rows_ref, cols_ref,
                   depth1_ref, mass1_ref, open_surf_ref, open_mass_ref):
    depth = depth_ref[...]
    bed = bed_ref[...]
    mass = mass_ref[...]
    cond = cond_ref[...]
    opened = wet_ref[...].astype(jnp.float32)
    surface = depth + bed
    tile_y, tile_x = depth.shape
    own = (surface, mass, cond, opened)
    row_id = lax.broadcasted_iota(jnp.int32, (tile_y, tile_x), 0)
    col_id = lax.broadcasted_iota(jnp.int32, (tile_y, tile_x), 1)
    rows = rows_ref[...]
    cols = cols_ref[...]

    def coeff(c_i, o_i, c_j, o_j):
        return 0.5 * (c_i + c_j) * o_i * o_j

    def ahead(field, axis):
        value = own[field]
        if axis == 0:
            return jnp.where(row_id == tile_y - 1, rows[4 + field : 5 + field, :], pltpu.roll(value, tile_y - 1, 0))
        return jnp.where(col_id == tile_x - 1, cols[:, 4 + field : 5 + field], pltpu.roll(value, tile_x - 1, 1))

    flux = []
    for axis in (0, 1):
        a = coeff(cond, opened, ahead(2, axis), ahead(3, axis))
        flux.append((a * (ahead(0, axis) - surface), a * (ahead(1, axis) - mass)))

    top = rows[0:4, :]
    left = cols[:, 0:4]
    a_top = coeff(cond[0:1, :], opened[0:1, :], top[2:3, :], top[3:4, :])
    a_left = coeff(cond[:, 0:1], opened[:, 0:1], left[:, 2:3], left[:, 3:4])
    edge_y = (a_top * (top[0:1, :] - surface[0:1, :]), a_top * (top[1:2, :] - mass[0:1, :]))
    edge_x = (a_left * (left[:, 0:1] - surface[:, 0:1]), a_left * (left[:, 1:2] - mass[:, 0:1]))

    def behind(k):
        from_y = jnp.where(row_id == 0, edge_y[k], -pltpu.roll(flux[0][k], 1, 0))
        from_x = jnp.where(col_id == 0, edge_x[k], -pltpu.roll(flux[1][k], 1, 1))
        return from_y, from_x

    gains = []
    for k in (0, 1):
        from_y, from_x = behind(k)
        gains.append(((flux[0][k] + from_y) + flux[1][k]) + from_x)
    depth1 = depth + gains[0]
    mass1 = (mass + gains[1]) * jnp.exp(-settle_ref[...])
    depth1_ref[...] = depth1
    mass1_ref[...] = mass1
    per_row = tile_x // 128
    surface1 = depth1 + bed
    for j in range(per_row):
        lanes = slice(j * 128, (j + 1) * 128)
        rows_j = pl.ds(j, tile_y, stride=per_row)
        open_j = opened[:, lanes]
        open_surf_ref[rows_j, :] = open_j * surface1[:, lanes]
        open_mass_ref[rows_j, :] = open_j * mass1[:, lanes]


def smooth_reach(values):
    left = jnp.concatenate([values[:, :1], values[:, :-1]], axis=1)
    right = jnp.concatenate([values[:, 1:], values[:, -1:]], axis=1)
    return values + 0.25 * (left - 2.0 * values + right)


def body(
    depth,
    bed,
    mass,
    conduct,
    settle,
    wet,
    link_block,
    link_owner,
    link_reach,
    link_coef,
    chan_phase,
    chan_conc,
    chan_area,
):
    tile_y, tile_x = depth.shape
    opened = wet.astype(jnp.float32)

    stacked = jnp.stack([depth + bed, mass, conduct, opened])
    top, bottom = halo_pair(stacked[:, tile_y - 1, :], stacked[:, 0, :], "row")
    left, right = halo_pair(stacked[:, :, tile_x - 1], stacked[:, :, 0], "col")
    rows = jnp.concatenate([top, bottom], axis=0)
    cols = jnp.concatenate([left, right], axis=0).T
    tile = jax.ShapeDtypeStruct((tile_y, tile_x), jnp.float32)
    vmem = pl.BlockSpec(memory_space=pltpu.VMEM)
    blocks = tile_y * tile_x // 128
    block_rows = jax.ShapeDtypeStruct((blocks, 128), jnp.float32)
    depth1, mass1, open_surf, open_mass = pl.pallas_call(
        stencil_kernel,
        out_shape=[tile, tile] + [block_rows] * 2,
        in_specs=[vmem] * 8,
        out_specs=[vmem] * 4,
        cost_estimate=pl.CostEstimate(
            flops=60 * tile_y * tile_x, transcendentals=tile_y * tile_x, bytes_accessed=40 * tile_y * tile_x
        ),
    )(depth, bed, mass, conduct, settle, wet, rows, cols)

    n_row = lax.axis_size("row")
    n_col = lax.axis_size("col")
    devices = n_row * n_col
    links_here = link_owner.shape[0]
    slot_cap = max(2, 2 * links_here // devices)
    target = link_owner[:, 0]
    owner_hot = (target[:, None] == jnp.arange(devices, dtype=jnp.int32)[None, :]).astype(jnp.int32)
    ranking = jnp.sum((jnp.cumsum(owner_hot, axis=0) - 1) * owner_hot, axis=1)
    slot_of = target * slot_cap + ranking
    slot_ids = jnp.arange(devices * slot_cap, dtype=jnp.int32)
    slot_hit = slot_of[None, :] == slot_ids[:, None]
    slot_block = jnp.max(jnp.where(slot_hit, link_block[None, :], -1), axis=1)
    block_ids = jnp.arange(blocks, dtype=jnp.int32)
    slot_hot = (slot_block[:, None] == block_ids[None, :]).astype(jnp.float32)
    coefs = jnp.maximum(jnp.max(jnp.where(slot_hit, link_coef[None, :], -1.0), axis=1), 0.0)
    payload = coefs[:, None] * jnp.dot(
        slot_hot, jnp.concatenate([open_surf, open_mass], axis=1), precision=lax.Precision.HIGHEST
    )
    tags = jnp.max(jnp.where(slot_hit, link_reach[None, :].astype(jnp.float32), -1.0), axis=1)
    meta = jnp.concatenate(
        [tags.reshape(devices, slot_cap), coefs.reshape(devices, slot_cap),
         jnp.zeros((devices, 128 - 2 * slot_cap), jnp.float32)],
        axis=1,
    )
    outgoing = jnp.concatenate([payload.reshape(devices, 2 * slot_cap * 128), meta], axis=1)
    arrived = lax.all_to_all(outgoing, ("row", "col"), split_axis=0, concat_axis=0, tiled=True)
    got = arrived[:, : 2 * slot_cap * 128].reshape(devices * slot_cap, 256)
    arrived_tags = arrived[:, 2 * slot_cap * 128 : 2 * slot_cap * 128 + slot_cap].reshape(devices * slot_cap)
    arrived_coef = arrived[:, 2 * slot_cap * 128 + slot_cap : 2 * slot_cap * 128 + 2 * slot_cap].reshape(
        devices * slot_cap
    )
    got_ws = got[:, :128]
    got_wm = got[:, 128:]
    got_w = jnp.where(got_wm > 0.0, arrived_coef[:, None], 0.0)
    reach_dev = chan_phase.shape[0]
    reach_hot = (arrived_tags[None, :] == jnp.arange(reach_dev, dtype=jnp.float32)[:, None]).astype(
        jnp.float32
    )
    totals = jnp.dot(
        reach_hot, jnp.concatenate([got_ws, got_wm, got_w], axis=1), precision=lax.Precision.HIGHEST
    )
    inflow = totals[:, :128]
    sediment = totals[:, 128:256]
    wet_sum = totals[:, 256:]
    phase_new = (chan_area * chan_phase + inflow) / (chan_area + wet_sum)
    conc_new = (chan_area * chan_conc + sediment) / (chan_area + wet_sum)
    phase_out = smooth_reach(phase_new)
    conc_out = smooth_reach(conc_new)
    reply = jnp.dot(
        reach_hot.T, jnp.concatenate([phase_out, conc_out], axis=1), precision=lax.Precision.HIGHEST
    )
    answered = lax.all_to_all(
        reply.reshape(devices, slot_cap, 256),
        ("row", "col"),
        split_axis=0,
        concat_axis=0,
        tiled=True,
    )
    own_rows = answered.reshape(devices * slot_cap, 256)[slot_of]
    surf_rows = (depth1 + bed).reshape(blocks, 128)[link_block]
    mass_rows = mass1.reshape(blocks, 128)[link_block]
    weight = link_coef[:, None] * opened.reshape(blocks, 128)[link_block]
    applied = jnp.concatenate(
        [
            0.5 * weight * (own_rows[:, :128] - surf_rows),
            0.5 * weight * (own_rows[:, 128:] - mass_rows),
        ],
        axis=1,
    )
    per_row = tile_x // 128
    row_ids = jnp.arange(tile_y, dtype=jnp.int32)[:, None]
    gained = [
        jnp.dot(
            (row_ids * per_row + j == link_block[None, :]).astype(jnp.float32),
            applied,
            precision=lax.Precision.HIGHEST,
        )
        for j in range(per_row)
    ]
    depth_out = depth1 + jnp.concatenate([g[:, :128] for g in gained], axis=1)
    mass_out = mass1 + jnp.concatenate([g[:, 128:] for g in gained], axis=1)
    return (depth_out, mass_out, phase_out, conc_out)


def solution(mesh):
    return jax.shard_map(
        body,
        mesh=mesh,
        in_specs=(
            P("row", "col"),
            P("row", "col"),
            P("row", "col"),
            P("row", "col"),
            P("row", "col"),
            P("row", "col"),
            P(("row", "col")),
            P(("row", "col"), None),
            P(("row", "col")),
            P(("row", "col")),
            P(("row", "col"), None),
            P(("row", "col"), None),
            P(("row", "col"), None),
        ),
        out_specs=(
            P("row", "col"),
            P("row", "col"),
            P(("row", "col"), None),
            P(("row", "col"), None),
        ),
        check_vma=False,
    )
```

```python
import jax
import jax.numpy as jnp
from jax import lax
from jax.experimental import pallas as pl
from jax.experimental.pallas import tpu as pltpu
from jax.sharding import PartitionSpec as P


def halo_pair(last, first, axis):
    count = lax.axis_size(axis)
    forward = [(i, i + 1) for i in range(count - 1)]
    backward = [(target, source) for source, target in forward]
    return lax.ppermute(last, axis, forward), lax.ppermute(first, axis, backward)


def edges_kernel(depth_top, depth_bottom, depth_left, depth_right, bed_top, bed_bottom, bed_left, bed_right,
                 mass_top, mass_bottom, mass_left, mass_right, cond_top, cond_bottom, cond_left, cond_right,
                 wet_top, wet_bottom, wet_left, wet_right, last_rows_ref, first_rows_ref, last_cols_ref,
                 first_cols_ref):
    def fields(d, b, m, c, w):
        return [d[...] + b[...], m[...], c[...], w[...].astype(jnp.float32)]

    top = fields(depth_top, bed_top, mass_top, cond_top, wet_top)
    bottom = fields(depth_bottom, bed_bottom, mass_bottom, cond_bottom, wet_bottom)
    left = fields(depth_left, bed_left, mass_left, cond_left, wet_left)
    right = fields(depth_right, bed_right, mass_right, cond_right, wet_right)
    for f in range(4):
        first_rows_ref[f : f + 1, :] = top[f][0:1, :]
        last_rows_ref[f : f + 1, :] = bottom[f][-1:, :]
        first_cols_ref[f : f + 1, :] = left[f].T[0:1, :]
        last_cols_ref[f : f + 1, :] = right[f].T[-1:, :]


def stencil_kernel(depth_ref, bed_ref, mass_ref, cond_ref, settle_ref, wet_ref, top_ref, bottom_ref, left_ref,
                   right_ref,
                   depth1_ref, mass1_ref, open_surf_ref, open_mass_ref):
    depth = depth_ref[...]
    bed = bed_ref[...]
    mass = mass_ref[...]
    cond = cond_ref[...]
    opened = wet_ref[...].astype(jnp.float32)
    surface = depth + bed
    tile_y, tile_x = depth.shape
    own = (surface, mass, cond, opened)
    row_id = lax.broadcasted_iota(jnp.int32, (tile_y, tile_x), 0)
    col_id = lax.broadcasted_iota(jnp.int32, (tile_y, tile_x), 1)
    rows = jnp.concatenate([top_ref[...], bottom_ref[...]], axis=0)
    sides = jnp.concatenate(
        [left_ref[...], right_ref[...], jnp.zeros((120, tile_y), jnp.float32)], axis=0
    )
    cols = sides.T

    def coeff(c_i, o_i, c_j, o_j):
        return 0.5 * (c_i + c_j) * o_i * o_j

    def ahead(field, axis):
        value = own[field]
        if axis == 0:
            return jnp.where(row_id == tile_y - 1, rows[4 + field : 5 + field, :], pltpu.roll(value, tile_y - 1, 0))
        return jnp.where(col_id == tile_x - 1, cols[:, 4 + field : 5 + field], pltpu.roll(value, tile_x - 1, 1))

    flux = []
    for axis in (0, 1):
        a = coeff(cond, opened, ahead(2, axis), ahead(3, axis))
        flux.append((a * (ahead(0, axis) - surface), a * (ahead(1, axis) - mass)))

    top = rows[0:4, :]
    left = cols[:, 0:4]
    a_top = coeff(cond[0:1, :], opened[0:1, :], top[2:3, :], top[3:4, :])
    a_left = coeff(cond[:, 0:1], opened[:, 0:1], left[:, 2:3], left[:, 3:4])
    edge_y = (a_top * (top[0:1, :] - surface[0:1, :]), a_top * (top[1:2, :] - mass[0:1, :]))
    edge_x = (a_left * (left[:, 0:1] - surface[:, 0:1]), a_left * (left[:, 1:2] - mass[:, 0:1]))

    def behind(k):
        from_y = jnp.where(row_id == 0, edge_y[k], -pltpu.roll(flux[0][k], 1, 0))
        from_x = jnp.where(col_id == 0, edge_x[k], -pltpu.roll(flux[1][k], 1, 1))
        return from_y, from_x

    gains = []
    for k in (0, 1):
        from_y, from_x = behind(k)
        gains.append(((flux[0][k] + from_y) + flux[1][k]) + from_x)
    depth1 = depth + gains[0]
    mass1 = (mass + gains[1]) * jnp.exp(-settle_ref[...])
    depth1_ref[...] = depth1
    mass1_ref[...] = mass1
    per_row = tile_x // 128
    surface1 = depth1 + bed
    for j in range(per_row):
        lanes = slice(j * 128, (j + 1) * 128)
        rows_j = pl.ds(j, tile_y, stride=per_row)
        open_j = opened[:, lanes]
        open_surf_ref[rows_j, :] = open_j * surface1[:, lanes]
        open_mass_ref[rows_j, :] = open_j * mass1[:, lanes]


def smooth_reach(values):
    left = jnp.concatenate([values[:, :1], values[:, :-1]], axis=1)
    right = jnp.concatenate([values[:, 1:], values[:, -1:]], axis=1)
    return values + 0.25 * (left - 2.0 * values + right)


def body(
    depth,
    bed,
    mass,
    conduct,
    settle,
    wet,
    link_block,
    link_owner,
    link_reach,
    link_coef,
    chan_phase,
    chan_conc,
    chan_area,
):
    tile_y, tile_x = depth.shape
    opened = wet.astype(jnp.float32)

    line = lambda n: jax.ShapeDtypeStruct((4, n), jnp.float32)

    def edge_specs():
        last_row = tile_y // 8 - 1
        last_col = tile_x // 128 - 1
        return [
            pl.BlockSpec((8, tile_x), lambda i: (0, 0)),
            pl.BlockSpec((8, tile_x), lambda i: (last_row, 0)),
            pl.BlockSpec((tile_y, 128), lambda i: (0, 0)),
            pl.BlockSpec((tile_y, 128), lambda i: (0, last_col)),
        ]

    last_rows, first_rows, last_cols, first_cols = pl.pallas_call(
        edges_kernel,
        out_shape=[line(tile_x), line(tile_x), line(tile_y), line(tile_y)],
        grid=(1,),
        in_specs=edge_specs() * 5,
        out_specs=[
            pl.BlockSpec((4, tile_x), lambda i: (0, 0)),
            pl.BlockSpec((4, tile_x), lambda i: (0, 0)),
            pl.BlockSpec((4, tile_y), lambda i: (0, 0)),
            pl.BlockSpec((4, tile_y), lambda i: (0, 0)),
        ],
    )(*[a for a in (depth, bed, mass, conduct, wet) for _ in range(4)])
    top, bottom = halo_pair(last_rows, first_rows, "row")
    left, right = halo_pair(last_cols, first_cols, "col")
    tile = jax.ShapeDtypeStruct((tile_y, tile_x), jnp.float32)
    vmem = pl.BlockSpec(memory_space=pltpu.VMEM)
    blocks = tile_y * tile_x // 128
    block_rows = jax.ShapeDtypeStruct((blocks, 128), jnp.float32)
    depth1, mass1, open_surf, open_mass = pl.pallas_call(
        stencil_kernel,
        out_shape=[tile, tile] + [block_rows] * 2,
        in_specs=[vmem] * 10,
        out_specs=[vmem] * 4,
        cost_estimate=pl.CostEstimate(
            flops=60 * tile_y * tile_x, transcendentals=tile_y * tile_x, bytes_accessed=40 * tile_y * tile_x
        ),
    )(depth, bed, mass, conduct, settle, wet, top, bottom, left, right)

    n_row = lax.axis_size("row")
    n_col = lax.axis_size("col")
    devices = n_row * n_col
    links_here = link_owner.shape[0]
    slot_cap = max(2, 2 * links_here // devices)
    target = link_owner[:, 0]
    owner_hot = (target[:, None] == jnp.arange(devices, dtype=jnp.int32)[None, :]).astype(jnp.int32)
    ranking = jnp.sum((jnp.cumsum(owner_hot, axis=0) - 1) * owner_hot, axis=1)
    slot_of = target * slot_cap + ranking
    slot_ids = jnp.arange(devices * slot_cap, dtype=jnp.int32)
    slot_hit = slot_of[None, :] == slot_ids[:, None]
    slot_block = jnp.max(jnp.where(slot_hit, link_block[None, :], -1), axis=1)
    block_ids = jnp.arange(blocks, dtype=jnp.int32)
    slot_hot = (slot_block[:, None] == block_ids[None, :]).astype(jnp.float32)
    coefs = jnp.maximum(jnp.max(jnp.where(slot_hit, link_coef[None, :], -1.0), axis=1), 0.0)
    payload = coefs[:, None] * jnp.dot(
        slot_hot, jnp.concatenate([open_surf, open_mass], axis=1), precision=lax.Precision.HIGHEST
    )
    tags = jnp.max(jnp.where(slot_hit, link_reach[None, :].astype(jnp.float32), -1.0), axis=1)
    meta = jnp.concatenate(
        [tags.reshape(devices, slot_cap), coefs.reshape(devices, slot_cap),
         jnp.zeros((devices, 128 - 2 * slot_cap), jnp.float32)],
        axis=1,
    )
    outgoing = jnp.concatenate([payload.reshape(devices, 2 * slot_cap * 128), meta], axis=1)
    arrived = lax.all_to_all(outgoing, ("row", "col"), split_axis=0, concat_axis=0, tiled=True)
    got = arrived[:, : 2 * slot_cap * 128].reshape(devices * slot_cap, 256)
    arrived_tags = arrived[:, 2 * slot_cap * 128 : 2 * slot_cap * 128 + slot_cap].reshape(devices * slot_cap)
    arrived_coef = arrived[:, 2 * slot_cap * 128 + slot_cap : 2 * slot_cap * 128 + 2 * slot_cap].reshape(
        devices * slot_cap
    )
    got_ws = got[:, :128]
    got_wm = got[:, 128:]
    got_w = jnp.where(got_wm > 0.0, arrived_coef[:, None], 0.0)
    reach_dev = chan_phase.shape[0]
    reach_hot = (arrived_tags[None, :] == jnp.arange(reach_dev, dtype=jnp.float32)[:, None]).astype(
        jnp.float32
    )
    totals = jnp.dot(
        reach_hot, jnp.concatenate([got_ws, got_wm, got_w], axis=1), precision=lax.Precision.HIGHEST
    )
    inflow = totals[:, :128]
    sediment = totals[:, 128:256]
    wet_sum = totals[:, 256:]
    phase_new = (chan_area * chan_phase + inflow) / (chan_area + wet_sum)
    conc_new = (chan_area * chan_conc + sediment) / (chan_area + wet_sum)
    phase_out = smooth_reach(phase_new)
    conc_out = smooth_reach(conc_new)
    reply = jnp.dot(
        reach_hot.T, jnp.concatenate([phase_out, conc_out], axis=1), precision=lax.Precision.HIGHEST
    )
    answered = lax.all_to_all(
        reply.reshape(devices, slot_cap, 256),
        ("row", "col"),
        split_axis=0,
        concat_axis=0,
        tiled=True,
    )
    own_rows = answered.reshape(devices * slot_cap, 256)[slot_of]
    surf_rows = (depth1 + bed).reshape(blocks, 128)[link_block]
    mass_rows = mass1.reshape(blocks, 128)[link_block]
    weight = link_coef[:, None] * opened.reshape(blocks, 128)[link_block]
    applied = jnp.concatenate(
        [
            0.5 * weight * (own_rows[:, :128] - surf_rows),
            0.5 * weight * (own_rows[:, 128:] - mass_rows),
        ],
        axis=1,
    )
    per_row = tile_x // 128
    row_ids = jnp.arange(tile_y, dtype=jnp.int32)[:, None]
    gained = [
        jnp.dot(
            (row_ids * per_row + j == link_block[None, :]).astype(jnp.float32),
            applied,
            precision=lax.Precision.HIGHEST,
        )
        for j in range(per_row)
    ]
    depth_out = depth1 + jnp.concatenate([g[:, :128] for g in gained], axis=1)
    mass_out = mass1 + jnp.concatenate([g[:, 128:] for g in gained], axis=1)
    return (depth_out, mass_out, phase_out, conc_out)


def solution(mesh):
    return jax.shard_map(
        body,
        mesh=mesh,
        in_specs=(
            P("row", "col"),
            P("row", "col"),
            P("row", "col"),
            P("row", "col"),
            P("row", "col"),
            P("row", "col"),
            P(("row", "col")),
            P(("row", "col"), None),
            P(("row", "col")),
            P(("row", "col")),
            P(("row", "col"), None),
            P(("row", "col"), None),
            P(("row", "col"), None),
        ),
        out_specs=(
            P("row", "col"),
            P("row", "col"),
            P(("row", "col"), None),
            P(("row", "col"), None),
        ),
        check_vma=False,
    )
```

```python
import jax
import jax.numpy as jnp
from jax import lax
from jax.experimental import pallas as pl
from jax.experimental.pallas import tpu as pltpu
from jax.sharding import PartitionSpec as P


def halo_pair(last, first, axis):
    count = lax.axis_size(axis)
    forward = [(i, i + 1) for i in range(count - 1)]
    backward = [(target, source) for source, target in forward]
    return lax.ppermute(last, axis, forward), lax.ppermute(first, axis, backward)


def stencil_kernel(depth_ref, bed_ref, mass_ref, cond_ref, settle_ref, wet_ref, rows_ref, cols_ref,
                   depth1_ref, mass1_ref, open_surf_ref, open_mass_ref):
    depth = depth_ref[...]
    bed = bed_ref[...]
    mass = mass_ref[...]
    cond = cond_ref[...]
    opened = wet_ref[...].astype(jnp.float32)
    surface = depth + bed
    tile_y, tile_x = depth.shape
    own = (surface, mass, cond, opened)
    row_id = lax.broadcasted_iota(jnp.int32, (tile_y, tile_x), 0)
    col_id = lax.broadcasted_iota(jnp.int32, (tile_y, tile_x), 1)
    rows = rows_ref[...]
    cols = cols_ref[...]

    def coeff(c_i, o_i, c_j, o_j):
        return 0.5 * (c_i + c_j) * o_i * o_j

    def ahead(field, axis):
        value = own[field]
        if axis == 0:
            return jnp.where(row_id == tile_y - 1, rows[4 + field : 5 + field, :], pltpu.roll(value, tile_y - 1, 0))
        return jnp.where(col_id == tile_x - 1, cols[:, 4 + field : 5 + field], pltpu.roll(value, tile_x - 1, 1))

    flux = []
    for axis in (0, 1):
        a = coeff(cond, opened, ahead(2, axis), ahead(3, axis))
        flux.append((a * (ahead(0, axis) - surface), a * (ahead(1, axis) - mass)))

    top = rows[0:4, :]
    left = cols[:, 0:4]
    a_top = coeff(cond[0:1, :], opened[0:1, :], top[2:3, :], top[3:4, :])
    a_left = coeff(cond[:, 0:1], opened[:, 0:1], left[:, 2:3], left[:, 3:4])
    edge_y = (a_top * (top[0:1, :] - surface[0:1, :]), a_top * (top[1:2, :] - mass[0:1, :]))
    edge_x = (a_left * (left[:, 0:1] - surface[:, 0:1]), a_left * (left[:, 1:2] - mass[:, 0:1]))

    def behind(k):
        from_y = jnp.where(row_id == 0, edge_y[k], -pltpu.roll(flux[0][k], 1, 0))
        from_x = jnp.where(col_id == 0, edge_x[k], -pltpu.roll(flux[1][k], 1, 1))
        return from_y, from_x

    gains = []
    for k in (0, 1):
        from_y, from_x = behind(k)
        gains.append(((flux[0][k] + from_y) + flux[1][k]) + from_x)
    depth1 = depth + gains[0]
    mass1 = (mass + gains[1]) * jnp.exp(-settle_ref[...])
    depth1_ref[...] = depth1
    mass1_ref[...] = mass1
    per_row = tile_x // 128
    surface1 = depth1 + bed
    for j in range(per_row):
        lanes = slice(j * 128, (j + 1) * 128)
        rows_j = pl.ds(j, tile_y, stride=per_row)
        open_j = opened[:, lanes]
        open_surf_ref[rows_j, :] = open_j * surface1[:, lanes]
        open_mass_ref[rows_j, :] = open_j * mass1[:, lanes]


def smooth_reach(values):
    left = jnp.concatenate([values[:, :1], values[:, :-1]], axis=1)
    right = jnp.concatenate([values[:, 1:], values[:, -1:]], axis=1)
    return values + 0.25 * (left - 2.0 * values + right)


def body(
    depth,
    bed,
    mass,
    conduct,
    settle,
    wet,
    link_block,
    link_owner,
    link_reach,
    link_coef,
    chan_phase,
    chan_conc,
    chan_area,
):
    tile_y, tile_x = depth.shape
    opened = wet.astype(jnp.float32)

    stacked = jnp.stack([depth + bed, mass, conduct, opened])
    top, bottom = halo_pair(stacked[:, tile_y - 1, :], stacked[:, 0, :], "row")
    left, right = halo_pair(stacked[:, :, tile_x - 1], stacked[:, :, 0], "col")
    rows = jnp.concatenate([top, bottom], axis=0)
    cols = jnp.concatenate([left, right], axis=0).T
    tile = jax.ShapeDtypeStruct((tile_y, tile_x), jnp.float32)
    vmem = pl.BlockSpec(memory_space=pltpu.VMEM)
    blocks = tile_y * tile_x // 128
    block_rows = jax.ShapeDtypeStruct((blocks, 128), jnp.float32)
    depth1, mass1, open_surf, open_mass = pl.pallas_call(
        stencil_kernel,
        out_shape=[tile, tile] + [block_rows] * 2,
        in_specs=[vmem] * 8,
        out_specs=[vmem] * 4,
        cost_estimate=pl.CostEstimate(
            flops=60 * tile_y * tile_x, transcendentals=tile_y * tile_x, bytes_accessed=40 * tile_y * tile_x
        ),
    )(depth, bed, mass, conduct, settle, wet, rows, cols)

    n_row = lax.axis_size("row")
    n_col = lax.axis_size("col")
    devices = n_row * n_col
    links_here = link_owner.shape[0]
    slot_cap = max(2, 2 * links_here // devices)
    target = link_owner[:, 0]
    owner_hot = (target[:, None] == jnp.arange(devices, dtype=jnp.int32)[None, :]).astype(jnp.int32)
    ranking = jnp.sum((jnp.cumsum(owner_hot, axis=0) - 1) * owner_hot, axis=1)
    slot_of = target * slot_cap + ranking
    slot_ids = jnp.arange(devices * slot_cap, dtype=jnp.int32)
    slot_hit = slot_of[None, :] == slot_ids[:, None]
    slot_block = jnp.max(jnp.where(slot_hit, link_block[None, :], -1), axis=1)
    block_ids = jnp.arange(blocks, dtype=jnp.int32)
    slot_hot = (slot_block[:, None] == block_ids[None, :]).astype(jnp.float32)
    coefs = jnp.maximum(jnp.max(jnp.where(slot_hit, link_coef[None, :], -1.0), axis=1), 0.0)
    payload = coefs[:, None] * jnp.dot(
        slot_hot, jnp.concatenate([open_surf, open_mass], axis=1), precision=lax.Precision.HIGHEST
    )
    tags = jnp.max(jnp.where(slot_hit, link_reach[None, :].astype(jnp.float32), -1.0), axis=1)
    meta = jnp.concatenate(
        [tags.reshape(devices, slot_cap), coefs.reshape(devices, slot_cap),
         jnp.zeros((devices, 128 - 2 * slot_cap), jnp.float32)],
        axis=1,
    )
    outgoing = jnp.concatenate(
        [payload.reshape(devices, 1, 2 * slot_cap * 128), meta.reshape(devices, 1, 128)], axis=2
    )
    arrived = lax.all_to_all(outgoing, ("row", "col"), split_axis=0, concat_axis=0, tiled=True)[:, 0, :]
    got = arrived[:, : 2 * slot_cap * 128].reshape(devices * slot_cap, 256)
    arrived_tags = arrived[:, 2 * slot_cap * 128 : 2 * slot_cap * 128 + slot_cap].reshape(devices * slot_cap)
    arrived_coef = arrived[:, 2 * slot_cap * 128 + slot_cap : 2 * slot_cap * 128 + 2 * slot_cap].reshape(
        devices * slot_cap
    )
    got_ws = got[:, :128]
    got_wm = got[:, 128:]
    got_w = jnp.where(got_wm > 0.0, arrived_coef[:, None], 0.0)
    reach_dev = chan_phase.shape[0]
    reach_hot = (arrived_tags[None, :] == jnp.arange(reach_dev, dtype=jnp.float32)[:, None]).astype(
        jnp.float32
    )
    totals = jnp.dot(
        reach_hot, jnp.concatenate([got_ws, got_wm, got_w], axis=1), precision=lax.Precision.HIGHEST
    )
    inflow = totals[:, :128]
    sediment = totals[:, 128:256]
    wet_sum = totals[:, 256:]
    phase_new = (chan_area * chan_phase + inflow) / (chan_area + wet_sum)
    conc_new = (chan_area * chan_conc + sediment) / (chan_area + wet_sum)
    phase_out = smooth_reach(phase_new)
    conc_out = smooth_reach(conc_new)
    reply = jnp.dot(
        reach_hot.T, jnp.concatenate([phase_out, conc_out], axis=1), precision=lax.Precision.HIGHEST
    )
    answered = lax.all_to_all(
        reply.reshape(devices, slot_cap, 256),
        ("row", "col"),
        split_axis=0,
        concat_axis=0,
        tiled=True,
    )
    own_rows = answered.reshape(devices * slot_cap, 256)[slot_of]
    surf_rows = (depth1 + bed).reshape(blocks, 128)[link_block]
    mass_rows = mass1.reshape(blocks, 128)[link_block]
    weight = link_coef[:, None] * opened.reshape(blocks, 128)[link_block]
    applied = jnp.concatenate(
        [
            0.5 * weight * (own_rows[:, :128] - surf_rows),
            0.5 * weight * (own_rows[:, 128:] - mass_rows),
        ],
        axis=1,
    )
    per_row = tile_x // 128
    row_ids = jnp.arange(tile_y, dtype=jnp.int32)[:, None]
    gained = [
        jnp.dot(
            (row_ids * per_row + j == link_block[None, :]).astype(jnp.float32),
            applied,
            precision=lax.Precision.HIGHEST,
        )
        for j in range(per_row)
    ]
    depth_out = depth1 + jnp.concatenate([g[:, :128] for g in gained], axis=1)
    mass_out = mass1 + jnp.concatenate([g[:, 128:] for g in gained], axis=1)
    return (depth_out, mass_out, phase_out, conc_out)


def solution(mesh):
    return jax.shard_map(
        body,
        mesh=mesh,
        in_specs=(
            P("row", "col"),
            P("row", "col"),
            P("row", "col"),
            P("row", "col"),
            P("row", "col"),
            P("row", "col"),
            P(("row", "col")),
            P(("row", "col"), None),
            P(("row", "col")),
            P(("row", "col")),
            P(("row", "col"), None),
            P(("row", "col"), None),
            P(("row", "col"), None),
        ),
        out_specs=(
            P("row", "col"),
            P("row", "col"),
            P(("row", "col"), None),
            P(("row", "col"), None),
        ),
        check_vma=False,
    )
```

```python
import jax
import jax.numpy as jnp
from jax import lax
from jax.experimental import pallas as pl
from jax.experimental.pallas import tpu as pltpu
from jax.sharding import PartitionSpec as P


def halo_pair(last, first, axis):
    count = lax.axis_size(axis)
    forward = [(i, i + 1) for i in range(count - 1)]
    backward = [(target, source) for source, target in forward]
    return lax.ppermute(last, axis, forward), lax.ppermute(first, axis, backward)


def stencil_kernel(depth_ref, bed_ref, mass_ref, cond_ref, settle_ref, wet_ref, rows_ref, cols_ref,
                   depth1_ref, mass1_ref, open_surf_ref, open_mass_ref):
    depth = depth_ref[...]
    bed = bed_ref[...]
    mass = mass_ref[...]
    cond = cond_ref[...]
    opened = wet_ref[...].astype(jnp.float32)
    surface = depth + bed
    tile_y, tile_x = depth.shape
    own = (surface, mass, cond, opened)
    row_id = lax.broadcasted_iota(jnp.int32, (tile_y, tile_x), 0)
    col_id = lax.broadcasted_iota(jnp.int32, (tile_y, tile_x), 1)
    rows = rows_ref[...]
    cols = cols_ref[...]

    def coeff(c_i, o_i, c_j, o_j):
        return 0.5 * (c_i + c_j) * o_i * o_j

    def ahead(field, axis):
        value = own[field]
        if axis == 0:
            return jnp.where(row_id == tile_y - 1, rows[4 + field : 5 + field, :], pltpu.roll(value, tile_y - 1, 0))
        return jnp.where(col_id == tile_x - 1, cols[:, 4 + field : 5 + field], pltpu.roll(value, tile_x - 1, 1))

    flux = []
    for axis in (0, 1):
        a = coeff(cond, opened, ahead(2, axis), ahead(3, axis))
        flux.append((a * (ahead(0, axis) - surface), a * (ahead(1, axis) - mass)))

    top = rows[0:4, :]
    left = cols[:, 0:4]
    a_top = coeff(cond[0:1, :], opened[0:1, :], top[2:3, :], top[3:4, :])
    a_left = coeff(cond[:, 0:1], opened[:, 0:1], left[:, 2:3], left[:, 3:4])
    edge_y = (a_top * (top[0:1, :] - surface[0:1, :]), a_top * (top[1:2, :] - mass[0:1, :]))
    edge_x = (a_left * (left[:, 0:1] - surface[:, 0:1]), a_left * (left[:, 1:2] - mass[:, 0:1]))

    def behind(k):
        from_y = jnp.where(row_id == 0, edge_y[k], -pltpu.roll(flux[0][k], 1, 0))
        from_x = jnp.where(col_id == 0, edge_x[k], -pltpu.roll(flux[1][k], 1, 1))
        return from_y, from_x

    gains = []
    for k in (0, 1):
        from_y, from_x = behind(k)
        gains.append(((flux[0][k] + from_y) + flux[1][k]) + from_x)
    depth1 = depth + gains[0]
    mass1 = (mass + gains[1]) * jnp.exp(-settle_ref[...])
    depth1_ref[...] = depth1
    mass1_ref[...] = mass1
    per_row = tile_x // 128
    surface1 = depth1 + bed
    for j in range(per_row):
        lanes = slice(j * 128, (j + 1) * 128)
        rows_j = pl.ds(j, tile_y, stride=per_row)
        open_j = opened[:, lanes]
        open_surf_ref[rows_j, :] = open_j * surface1[:, lanes]
        open_mass_ref[rows_j, :] = open_j * mass1[:, lanes]


def smooth_reach(values):
    left = jnp.concatenate([values[:, :1], values[:, :-1]], axis=1)
    right = jnp.concatenate([values[:, 1:], values[:, -1:]], axis=1)
    return values + 0.25 * (left - 2.0 * values + right)


def body(
    depth,
    bed,
    mass,
    conduct,
    settle,
    wet,
    link_block,
    link_owner,
    link_reach,
    link_coef,
    chan_phase,
    chan_conc,
    chan_area,
):
    tile_y, tile_x = depth.shape
    opened = wet.astype(jnp.float32)

    stacked = jnp.stack([depth + bed, mass, conduct, opened])
    top, bottom = halo_pair(stacked[:, tile_y - 1, :], stacked[:, 0, :], "row")
    left, right = halo_pair(stacked[:, :, tile_x - 1], stacked[:, :, 0], "col")
    rows = jnp.concatenate([top, bottom], axis=0)
    cols = jnp.concatenate([left, right], axis=0).T
    tile = jax.ShapeDtypeStruct((tile_y, tile_x), jnp.float32)
    vmem = pl.BlockSpec(memory_space=pltpu.VMEM)
    blocks = tile_y * tile_x // 128
    block_rows = jax.ShapeDtypeStruct((blocks, 128), jnp.float32)
    depth1, mass1, open_surf, open_mass = pl.pallas_call(
        stencil_kernel,
        out_shape=[tile, tile] + [block_rows] * 2,
        in_specs=[vmem] * 8,
        out_specs=[vmem] * 4,
        cost_estimate=pl.CostEstimate(
            flops=60 * tile_y * tile_x, transcendentals=tile_y * tile_x, bytes_accessed=40 * tile_y * tile_x
        ),
    )(depth, bed, mass, conduct, settle, wet, rows, cols)

    n_row = lax.axis_size("row")
    n_col = lax.axis_size("col")
    devices = n_row * n_col
    links_here = link_owner.shape[0]
    slot_cap = max(2, 2 * links_here // devices)
    target = link_owner[:, 0]
    owner_hot = (target[:, None] == jnp.arange(devices, dtype=jnp.int32)[None, :]).astype(jnp.int32)
    ranking = jnp.sum((jnp.cumsum(owner_hot, axis=0) - 1) * owner_hot, axis=1)
    slot_of = target * slot_cap + ranking
    slot_ids = jnp.arange(devices * slot_cap, dtype=jnp.int32)
    slot_hit = slot_of[None, :] == slot_ids[:, None]
    slot_block = jnp.max(jnp.where(slot_hit, link_block[None, :], -1), axis=1)
    block_ids = jnp.arange(blocks, dtype=jnp.int32)
    slot_hot = (slot_block[:, None] == block_ids[None, :]).astype(jnp.float32)
    coefs = jnp.maximum(jnp.max(jnp.where(slot_hit, link_coef[None, :], -1.0), axis=1), 0.0)
    payload = coefs[:, None] * jnp.dot(
        slot_hot, jnp.concatenate([open_surf, open_mass], axis=1), precision=lax.Precision.HIGHEST
    )
    tags = jnp.max(jnp.where(slot_hit, link_reach[None, :].astype(jnp.float32), -1.0), axis=1)
    meta = jnp.concatenate(
        [tags.reshape(devices, slot_cap), coefs.reshape(devices, slot_cap),
         jnp.zeros((devices, 128 - 2 * slot_cap), jnp.float32)],
        axis=1,
    )
    outgoing = jnp.concatenate([payload.reshape(devices, 2 * slot_cap * 128), meta], axis=1)
    arrived = lax.all_to_all(outgoing, ("row", "col"), split_axis=0, concat_axis=0, tiled=True)
    got = arrived[:, : 2 * slot_cap * 128].reshape(devices * slot_cap, 256)
    arrived_tags = arrived[:, 2 * slot_cap * 128 : 2 * slot_cap * 128 + slot_cap].reshape(devices * slot_cap)
    arrived_coef = arrived[:, 2 * slot_cap * 128 + slot_cap : 2 * slot_cap * 128 + 2 * slot_cap].reshape(
        devices * slot_cap
    )
    got_ws = got[:, :128]
    got_wm = got[:, 128:]
    got_w = jnp.where(got_wm > 0.0, arrived_coef[:, None], 0.0)
    reach_dev = chan_phase.shape[0]
    reach_hot = (arrived_tags[None, :] == jnp.arange(reach_dev, dtype=jnp.float32)[:, None]).astype(
        jnp.float32
    )
    totals = jnp.dot(
        reach_hot, jnp.concatenate([got_ws, got_wm, got_w], axis=1), precision=lax.Precision.HIGHEST
    )
    inflow = totals[:, :128]
    sediment = totals[:, 128:256]
    wet_sum = totals[:, 256:]
    phase_new = (chan_area * chan_phase + inflow) / (chan_area + wet_sum)
    conc_new = (chan_area * chan_conc + sediment) / (chan_area + wet_sum)
    phase_out = smooth_reach(phase_new)
    conc_out = smooth_reach(conc_new)
    reply = jnp.dot(
        reach_hot.T, jnp.concatenate([phase_out, conc_out], axis=1), precision=lax.Precision.HIGHEST
    )
    answered = lax.all_to_all(
        reply.reshape(devices, slot_cap, 256),
        ("row", "col"),
        split_axis=0,
        concat_axis=0,
        tiled=True,
    )
    own_rows = answered.reshape(devices * slot_cap, 256)[slot_of]
    surf_rows = (depth1 + bed).reshape(blocks, 128)[link_block]
    mass_rows = mass1.reshape(blocks, 128)[link_block]
    weight = link_coef[:, None] * opened.reshape(blocks, 128)[link_block]
    applied = jnp.concatenate(
        [
            0.5 * weight * (own_rows[:, :128] - surf_rows),
            0.5 * weight * (own_rows[:, 128:] - mass_rows),
        ],
        axis=1,
    )
    per_row = tile_x // 128
    row_ids = jnp.arange(tile_y, dtype=jnp.int32)[:, None]
    column_ids = jnp.arange(per_row, dtype=jnp.int32)[:, None, None]
    block_hot = (row_ids[None] * per_row + column_ids == link_block[None, None, :]).astype(jnp.float32)
    gained = jnp.einsum("jyl,lc->jyc", block_hot, applied, precision=lax.Precision.HIGHEST)
    depth_out = depth1 + jnp.concatenate([gained[j, :, :128] for j in range(per_row)], axis=1)
    mass_out = mass1 + jnp.concatenate([gained[j, :, 128:] for j in range(per_row)], axis=1)
    return (depth_out, mass_out, phase_out, conc_out)


def solution(mesh):
    return jax.shard_map(
        body,
        mesh=mesh,
        in_specs=(
            P("row", "col"),
            P("row", "col"),
            P("row", "col"),
            P("row", "col"),
            P("row", "col"),
            P("row", "col"),
            P(("row", "col")),
            P(("row", "col"), None),
            P(("row", "col")),
            P(("row", "col")),
            P(("row", "col"), None),
            P(("row", "col"), None),
            P(("row", "col"), None),
        ),
        out_specs=(
            P("row", "col"),
            P("row", "col"),
            P(("row", "col"), None),
            P(("row", "col"), None),
        ),
        check_vma=False,
    )
```

```python
import jax
import jax.numpy as jnp
from jax import lax
from jax.experimental import pallas as pl
from jax.experimental.pallas import tpu as pltpu
from jax.sharding import PartitionSpec as P


def halo_pair(last, first, axis):
    count = lax.axis_size(axis)
    forward = [(i, i + 1) for i in range(count - 1)]
    backward = [(target, source) for source, target in forward]
    return lax.ppermute(last, axis, forward), lax.ppermute(first, axis, backward)


def stencil_kernel(depth_ref, bed_ref, mass_ref, cond_ref, settle_ref, wet_ref, rows_ref, cols_ref,
                   depth1_ref, mass1_ref, open_surf_ref, open_mass_ref):
    depth = depth_ref[...]
    bed = bed_ref[...]
    mass = mass_ref[...]
    cond = cond_ref[...]
    opened = wet_ref[...].astype(jnp.float32)
    surface = depth + bed
    tile_y, tile_x = depth.shape
    own = (surface, mass, cond, opened)
    row_id = lax.broadcasted_iota(jnp.int32, (tile_y, tile_x), 0)
    col_id = lax.broadcasted_iota(jnp.int32, (tile_y, tile_x), 1)
    rows = rows_ref[...]
    cols = cols_ref[...]

    def coeff(c_i, o_i, c_j, o_j):
        return 0.5 * (c_i + c_j) * o_i * o_j

    def ahead(field, axis):
        value = own[field]
        if axis == 0:
            return jnp.where(row_id == tile_y - 1, rows[4 + field : 5 + field, :], pltpu.roll(value, tile_y - 1, 0))
        return jnp.where(col_id == tile_x - 1, cols[:, 4 + field : 5 + field], pltpu.roll(value, tile_x - 1, 1))

    flux = []
    for axis in (0, 1):
        a = coeff(cond, opened, ahead(2, axis), ahead(3, axis))
        flux.append((a * (ahead(0, axis) - surface), a * (ahead(1, axis) - mass)))

    top = rows[0:4, :]
    left = cols[:, 0:4]
    a_top = coeff(cond[0:1, :], opened[0:1, :], top[2:3, :], top[3:4, :])
    a_left = coeff(cond[:, 0:1], opened[:, 0:1], left[:, 2:3], left[:, 3:4])
    edge_y = (a_top * (top[0:1, :] - surface[0:1, :]), a_top * (top[1:2, :] - mass[0:1, :]))
    edge_x = (a_left * (left[:, 0:1] - surface[:, 0:1]), a_left * (left[:, 1:2] - mass[:, 0:1]))

    def behind(k):
        from_y = jnp.where(row_id == 0, edge_y[k], -pltpu.roll(flux[0][k], 1, 0))
        from_x = jnp.where(col_id == 0, edge_x[k], -pltpu.roll(flux[1][k], 1, 1))
        return from_y, from_x

    gains = []
    for k in (0, 1):
        from_y, from_x = behind(k)
        gains.append(((flux[0][k] + from_y) + flux[1][k]) + from_x)
    depth1 = depth + gains[0]
    mass1 = (mass + gains[1]) * jnp.exp(-settle_ref[...])
    depth1_ref[...] = depth1
    mass1_ref[...] = mass1
    per_row = tile_x // 128
    surface1 = depth1 + bed
    for j in range(per_row):
        lanes = slice(j * 128, (j + 1) * 128)
        rows_j = pl.ds(j, tile_y, stride=per_row)
        open_j = opened[:, lanes]
        open_surf_ref[rows_j, :] = open_j * surface1[:, lanes]
        open_mass_ref[rows_j, :] = open_j * mass1[:, lanes]


def owner_kernel(ws_ref, wm_ref, w_ref, hot_ref, hot_t_ref, phase_ref, conc_ref, area_ref,
                 phase_out_ref, conc_out_ref, reply_ref):
    gathered = jnp.concatenate([ws_ref[...], wm_ref[...], w_ref[...]], axis=1)
    totals = jnp.dot(hot_ref[...], gathered, precision=lax.Precision.HIGHEST,
                     preferred_element_type=jnp.float32)
    sections = phase_ref.shape[1]
    inflow = totals[:, :sections]
    sediment = totals[:, sections : 2 * sections]
    wet_sum = totals[:, 2 * sections :]
    area = area_ref[...]
    lane = lax.broadcasted_iota(jnp.int32, area.shape, 1)

    def smooth(values):
        left = jnp.where(lane == 0, values, pltpu.roll(values, 1, 1))
        right = jnp.where(lane == sections - 1, values, pltpu.roll(values, sections - 1, 1))
        return values + 0.25 * (left - 2.0 * values + right)

    phase_out = smooth((area * phase_ref[...] + inflow) / (area + wet_sum))
    conc_out = smooth((area * conc_ref[...] + sediment) / (area + wet_sum))
    phase_out_ref[...] = phase_out
    conc_out_ref[...] = conc_out
    reply_ref[...] = jnp.dot(hot_t_ref[...], jnp.concatenate([phase_out, conc_out], axis=1),
                             precision=lax.Precision.HIGHEST, preferred_element_type=jnp.float32)


def smooth_reach(values):
    left = jnp.concatenate([values[:, :1], values[:, :-1]], axis=1)
    right = jnp.concatenate([values[:, 1:], values[:, -1:]], axis=1)
    return values + 0.25 * (left - 2.0 * values + right)


def body(
    depth,
    bed,
    mass,
    conduct,
    settle,
    wet,
    link_block,
    link_owner,
    link_reach,
    link_coef,
    chan_phase,
    chan_conc,
    chan_area,
):
    tile_y, tile_x = depth.shape
    opened = wet.astype(jnp.float32)

    stacked = jnp.stack([depth + bed, mass, conduct, opened])
    top, bottom = halo_pair(stacked[:, tile_y - 1, :], stacked[:, 0, :], "row")
    left, right = halo_pair(stacked[:, :, tile_x - 1], stacked[:, :, 0], "col")
    rows = jnp.concatenate([top, bottom], axis=0)
    cols = jnp.concatenate([left, right], axis=0).T
    tile = jax.ShapeDtypeStruct((tile_y, tile_x), jnp.float32)
    vmem = pl.BlockSpec(memory_space=pltpu.VMEM)
    blocks = tile_y * tile_x // 128
    block_rows = jax.ShapeDtypeStruct((blocks, 128), jnp.float32)
    depth1, mass1, open_surf, open_mass = pl.pallas_call(
        stencil_kernel,
        out_shape=[tile, tile] + [block_rows] * 2,
        in_specs=[vmem] * 8,
        out_specs=[vmem] * 4,
        cost_estimate=pl.CostEstimate(
            flops=60 * tile_y * tile_x, transcendentals=tile_y * tile_x, bytes_accessed=40 * tile_y * tile_x
        ),
    )(depth, bed, mass, conduct, settle, wet, rows, cols)

    n_row = lax.axis_size("row")
    n_col = lax.axis_size("col")
    devices = n_row * n_col
    links_here = link_owner.shape[0]
    slot_cap = max(2, 2 * links_here // devices)
    target = link_owner[:, 0]
    owner_hot = (target[:, None] == jnp.arange(devices, dtype=jnp.int32)[None, :]).astype(jnp.int32)
    ranking = jnp.sum((jnp.cumsum(owner_hot, axis=0) - 1) * owner_hot, axis=1)
    slot_of = target * slot_cap + ranking
    slot_ids = jnp.arange(devices * slot_cap, dtype=jnp.int32)
    slot_hit = slot_of[None, :] == slot_ids[:, None]
    slot_block = jnp.max(jnp.where(slot_hit, link_block[None, :], -1), axis=1)
    block_ids = jnp.arange(blocks, dtype=jnp.int32)
    slot_hot = (slot_block[:, None] == block_ids[None, :]).astype(jnp.float32)
    coefs = jnp.maximum(jnp.max(jnp.where(slot_hit, link_coef[None, :], -1.0), axis=1), 0.0)
    payload = coefs[:, None] * jnp.dot(
        slot_hot, jnp.concatenate([open_surf, open_mass], axis=1), precision=lax.Precision.HIGHEST
    )
    tags = jnp.max(jnp.where(slot_hit, link_reach[None, :].astype(jnp.float32), -1.0), axis=1)
    meta = jnp.concatenate(
        [tags.reshape(devices, slot_cap), coefs.reshape(devices, slot_cap),
         jnp.zeros((devices, 128 - 2 * slot_cap), jnp.float32)],
        axis=1,
    )
    outgoing = jnp.concatenate([payload.reshape(devices, 2 * slot_cap * 128), meta], axis=1)
    arrived = lax.all_to_all(outgoing, ("row", "col"), split_axis=0, concat_axis=0, tiled=True)
    got = arrived[:, : 2 * slot_cap * 128].reshape(devices * slot_cap, 256)
    arrived_tags = arrived[:, 2 * slot_cap * 128 : 2 * slot_cap * 128 + slot_cap].reshape(devices * slot_cap)
    arrived_coef = arrived[:, 2 * slot_cap * 128 + slot_cap : 2 * slot_cap * 128 + 2 * slot_cap].reshape(
        devices * slot_cap
    )
    got_ws = got[:, :128]
    got_wm = got[:, 128:]
    got_w = jnp.where(got_wm > 0.0, arrived_coef[:, None], 0.0)
    reach_dev = chan_phase.shape[0]
    reach_ids = jnp.arange(reach_dev, dtype=jnp.float32)
    reach_hot = (arrived_tags[None, :] == reach_ids[:, None]).astype(jnp.float32)
    reach_hot_t = (arrived_tags[:, None] == reach_ids[None, :]).astype(jnp.float32)
    reach_rows = jax.ShapeDtypeStruct(chan_phase.shape, jnp.float32)
    phase_out, conc_out, reply = pl.pallas_call(
        owner_kernel,
        out_shape=[reach_rows, reach_rows, jax.ShapeDtypeStruct((devices * slot_cap, 256), jnp.float32)],
        in_specs=[vmem] * 8,
        out_specs=[vmem] * 3,
    )(got_ws, got_wm, got_w, reach_hot, reach_hot_t, chan_phase, chan_conc, chan_area)
    answered = lax.all_to_all(
        reply.reshape(devices, slot_cap, 256),
        ("row", "col"),
        split_axis=0,
        concat_axis=0,
        tiled=True,
    )
    own_rows = answered.reshape(devices * slot_cap, 256)[slot_of]
    surf_rows = (depth1 + bed).reshape(blocks, 128)[link_block]
    mass_rows = mass1.reshape(blocks, 128)[link_block]
    weight = link_coef[:, None] * opened.reshape(blocks, 128)[link_block]
    applied = jnp.concatenate(
        [
            0.5 * weight * (own_rows[:, :128] - surf_rows),
            0.5 * weight * (own_rows[:, 128:] - mass_rows),
        ],
        axis=1,
    )
    per_row = tile_x // 128
    row_ids = jnp.arange(tile_y, dtype=jnp.int32)[:, None]
    column_ids = jnp.arange(per_row, dtype=jnp.int32)[:, None, None]
    block_hot = (row_ids[None] * per_row + column_ids == link_block[None, None, :]).astype(jnp.float32)
    gained = jnp.einsum("jyl,lc->jyc", block_hot, applied, precision=lax.Precision.HIGHEST)
    depth_out = depth1 + jnp.concatenate([gained[j, :, :128] for j in range(per_row)], axis=1)
    mass_out = mass1 + jnp.concatenate([gained[j, :, 128:] for j in range(per_row)], axis=1)
    return (depth_out, mass_out, phase_out, conc_out)


def solution(mesh):
    return jax.shard_map(
        body,
        mesh=mesh,
        in_specs=(
            P("row", "col"),
            P("row", "col"),
            P("row", "col"),
            P("row", "col"),
            P("row", "col"),
            P("row", "col"),
            P(("row", "col")),
            P(("row", "col"), None),
            P(("row", "col")),
            P(("row", "col")),
            P(("row", "col"), None),
            P(("row", "col"), None),
            P(("row", "col"), None),
        ),
        out_specs=(
            P("row", "col"),
            P("row", "col"),
            P(("row", "col"), None),
            P(("row", "col"), None),
        ),
        check_vma=False,
    )
```

```python
import jax
import jax.numpy as jnp
from jax import lax
from jax.experimental import pallas as pl
from jax.experimental.pallas import tpu as pltpu
from jax.sharding import PartitionSpec as P


def halo_pair(last, first, axis):
    count = lax.axis_size(axis)
    forward = [(i, i + 1) for i in range(count - 1)]
    backward = [(target, source) for source, target in forward]
    return lax.ppermute(last, axis, forward), lax.ppermute(first, axis, backward)


def stencil_kernel(depth_ref, bed_ref, mass_ref, cond_ref, settle_ref, wet_ref, rows_ref, cols_ref,
                   depth1_ref, mass1_ref, open_surf_ref, open_mass_ref):
    depth = depth_ref[...]
    bed = bed_ref[...]
    mass = mass_ref[...]
    cond = cond_ref[...]
    opened = wet_ref[...].astype(jnp.float32)
    surface = depth + bed
    tile_y, tile_x = depth.shape
    own = (surface, mass, cond, opened)
    row_id = lax.broadcasted_iota(jnp.int32, (tile_y, tile_x), 0)
    col_id = lax.broadcasted_iota(jnp.int32, (tile_y, tile_x), 1)
    rows = rows_ref[...]
    cols = cols_ref[...]

    def coeff(c_i, o_i, c_j, o_j):
        return 0.5 * (c_i + c_j) * o_i * o_j

    def ahead(field, axis):
        value = own[field]
        if axis == 0:
            return jnp.where(row_id == tile_y - 1, rows[4 + field : 5 + field, :], pltpu.roll(value, tile_y - 1, 0))
        return jnp.where(col_id == tile_x - 1, cols[:, 4 + field : 5 + field], pltpu.roll(value, tile_x - 1, 1))

    flux = []
    for axis in (0, 1):
        a = coeff(cond, opened, ahead(2, axis), ahead(3, axis))
        flux.append((a * (ahead(0, axis) - surface), a * (ahead(1, axis) - mass)))

    top = rows[0:4, :]
    left = cols[:, 0:4]
    a_top = coeff(cond[0:1, :], opened[0:1, :], top[2:3, :], top[3:4, :])
    a_left = coeff(cond[:, 0:1], opened[:, 0:1], left[:, 2:3], left[:, 3:4])
    edge_y = (a_top * (top[0:1, :] - surface[0:1, :]), a_top * (top[1:2, :] - mass[0:1, :]))
    edge_x = (a_left * (left[:, 0:1] - surface[:, 0:1]), a_left * (left[:, 1:2] - mass[:, 0:1]))

    def behind(k):
        from_y = jnp.where(row_id == 0, edge_y[k], -pltpu.roll(flux[0][k], 1, 0))
        from_x = jnp.where(col_id == 0, edge_x[k], -pltpu.roll(flux[1][k], 1, 1))
        return from_y, from_x

    gains = []
    for k in (0, 1):
        from_y, from_x = behind(k)
        gains.append(((flux[0][k] + from_y) + flux[1][k]) + from_x)
    depth1 = depth + gains[0]
    mass1 = (mass + gains[1]) * jnp.exp(-settle_ref[...])
    depth1_ref[...] = depth1
    mass1_ref[...] = mass1
    per_row = tile_x // 128
    surface1 = depth1 + bed
    for j in range(per_row):
        lanes = slice(j * 128, (j + 1) * 128)
        rows_j = pl.ds(j, tile_y, stride=per_row)
        open_j = opened[:, lanes]
        open_surf_ref[rows_j, :] = open_j * surface1[:, lanes]
        open_mass_ref[rows_j, :] = open_j * mass1[:, lanes]


def smooth_reach(values):
    left = jnp.concatenate([values[:, :1], values[:, :-1]], axis=1)
    right = jnp.concatenate([values[:, 1:], values[:, -1:]], axis=1)
    return values + 0.25 * (left - 2.0 * values + right)


def body(
    depth,
    bed,
    mass,
    conduct,
    settle,
    wet,
    link_block,
    link_owner,
    link_reach,
    link_coef,
    chan_phase,
    chan_conc,
    chan_area,
):
    tile_y, tile_x = depth.shape
    opened = wet.astype(jnp.float32)

    stacked = jnp.stack([depth + bed, mass, conduct, opened])
    top, bottom = halo_pair(stacked[:, tile_y - 1, :], stacked[:, 0, :], "row")
    left, right = halo_pair(stacked[:, :, tile_x - 1], stacked[:, :, 0], "col")
    rows = jnp.concatenate([top, bottom], axis=0)
    cols = jnp.concatenate([left, right], axis=0).T
    tile = jax.ShapeDtypeStruct((tile_y, tile_x), jnp.float32)
    vmem = pl.BlockSpec(memory_space=pltpu.VMEM)
    blocks = tile_y * tile_x // 128
    block_rows = jax.ShapeDtypeStruct((blocks, 128), jnp.float32)
    depth1, mass1, open_surf, open_mass = pl.pallas_call(
        stencil_kernel,
        out_shape=[tile, tile] + [block_rows] * 2,
        in_specs=[vmem] * 8,
        out_specs=[vmem] * 4,
        cost_estimate=pl.CostEstimate(
            flops=60 * tile_y * tile_x, transcendentals=tile_y * tile_x, bytes_accessed=40 * tile_y * tile_x
        ),
    )(depth, bed, mass, conduct, settle, wet, rows, cols)

    n_row = lax.axis_size("row")
    n_col = lax.axis_size("col")
    devices = n_row * n_col
    links_here = link_owner.shape[0]
    slot_cap = max(2, 2 * links_here // devices)
    target = link_owner[:, 0]
    owner_hot = (target[:, None] == jnp.arange(devices, dtype=jnp.int32)[None, :]).astype(jnp.int32)
    ranking = jnp.sum((jnp.cumsum(owner_hot, axis=0) - 1) * owner_hot, axis=1)
    slot_of = target * slot_cap + ranking
    slot_ids = jnp.arange(devices * slot_cap, dtype=jnp.int32)
    slot_hit = slot_of[None, :] == slot_ids[:, None]
    slot_block = jnp.max(jnp.where(slot_hit, link_block[None, :], -1), axis=1)
    block_ids = jnp.arange(blocks, dtype=jnp.int32)
    slot_hot = (slot_block[:, None] == block_ids[None, :]).astype(jnp.float32)
    coefs = jnp.maximum(jnp.max(jnp.where(slot_hit, link_coef[None, :], -1.0), axis=1), 0.0)
    payload = coefs[:, None] * jnp.dot(
        slot_hot, jnp.concatenate([open_surf, open_mass], axis=1), precision=lax.Precision.HIGH
    )
    tags = jnp.max(jnp.where(slot_hit, link_reach[None, :].astype(jnp.float32), -1.0), axis=1)
    meta = jnp.concatenate(
        [tags.reshape(devices, slot_cap), coefs.reshape(devices, slot_cap),
         jnp.zeros((devices, 128 - 2 * slot_cap), jnp.float32)],
        axis=1,
    )
    outgoing = jnp.concatenate([payload.reshape(devices, 2 * slot_cap * 128), meta], axis=1)
    arrived = lax.all_to_all(outgoing, ("row", "col"), split_axis=0, concat_axis=0, tiled=True)
    got = arrived[:, : 2 * slot_cap * 128].reshape(devices * slot_cap, 256)
    arrived_tags = arrived[:, 2 * slot_cap * 128 : 2 * slot_cap * 128 + slot_cap].reshape(devices * slot_cap)
    arrived_coef = arrived[:, 2 * slot_cap * 128 + slot_cap : 2 * slot_cap * 128 + 2 * slot_cap].reshape(
        devices * slot_cap
    )
    got_ws = got[:, :128]
    got_wm = got[:, 128:]
    got_w = jnp.where(got_wm > 0.0, arrived_coef[:, None], 0.0)
    reach_dev = chan_phase.shape[0]
    reach_hot = (arrived_tags[None, :] == jnp.arange(reach_dev, dtype=jnp.float32)[:, None]).astype(
        jnp.float32
    )
    totals = jnp.dot(
        reach_hot, jnp.concatenate([got_ws, got_wm, got_w], axis=1), precision=lax.Precision.HIGHEST
    )
    inflow = totals[:, :128]
    sediment = totals[:, 128:256]
    wet_sum = totals[:, 256:]
    phase_new = (chan_area * chan_phase + inflow) / (chan_area + wet_sum)
    conc_new = (chan_area * chan_conc + sediment) / (chan_area + wet_sum)
    phase_out = smooth_reach(phase_new)
    conc_out = smooth_reach(conc_new)
    reply = jnp.dot(
        reach_hot.T, jnp.concatenate([phase_out, conc_out], axis=1), precision=lax.Precision.HIGH
    )
    answered = lax.all_to_all(
        reply.reshape(devices, slot_cap, 256),
        ("row", "col"),
        split_axis=0,
        concat_axis=0,
        tiled=True,
    )
    own_rows = answered.reshape(devices * slot_cap, 256)[slot_of]
    surf_rows = (depth1 + bed).reshape(blocks, 128)[link_block]
    mass_rows = mass1.reshape(blocks, 128)[link_block]
    weight = link_coef[:, None] * opened.reshape(blocks, 128)[link_block]
    applied = jnp.concatenate(
        [
            0.5 * weight * (own_rows[:, :128] - surf_rows),
            0.5 * weight * (own_rows[:, 128:] - mass_rows),
        ],
        axis=1,
    )
    per_row = tile_x // 128
    row_ids = jnp.arange(tile_y, dtype=jnp.int32)[:, None]
    column_ids = jnp.arange(per_row, dtype=jnp.int32)[:, None, None]
    block_hot = (row_ids[None] * per_row + column_ids == link_block[None, None, :]).astype(jnp.float32)
    gained = jnp.einsum("jyl,lc->jyc", block_hot, applied, precision=lax.Precision.HIGH)
    depth_out = depth1 + jnp.concatenate([gained[j, :, :128] for j in range(per_row)], axis=1)
    mass_out = mass1 + jnp.concatenate([gained[j, :, 128:] for j in range(per_row)], axis=1)
    return (depth_out, mass_out, phase_out, conc_out)


def solution(mesh):
    return jax.shard_map(
        body,
        mesh=mesh,
        in_specs=(
            P("row", "col"),
            P("row", "col"),
            P("row", "col"),
            P("row", "col"),
            P("row", "col"),
            P("row", "col"),
            P(("row", "col")),
            P(("row", "col"), None),
            P(("row", "col")),
            P(("row", "col")),
            P(("row", "col"), None),
            P(("row", "col"), None),
            P(("row", "col"), None),
        ),
        out_specs=(
            P("row", "col"),
            P("row", "col"),
            P(("row", "col"), None),
            P(("row", "col"), None),
        ),
        check_vma=False,
    )
```

```python
import jax
import jax.numpy as jnp
from jax import lax
from jax.experimental import pallas as pl
from jax.experimental.pallas import tpu as pltpu
from jax.sharding import PartitionSpec as P


def halo_pair(last, first, axis):
    count = lax.axis_size(axis)
    forward = [(i, i + 1) for i in range(count - 1)]
    backward = [(target, source) for source, target in forward]
    return lax.ppermute(last, axis, forward), lax.ppermute(first, axis, backward)


def stencil_kernel(depth_ref, bed_ref, mass_ref, cond_ref, settle_ref, wet_ref, rows_ref, cols_ref,
                   depth1_ref, mass1_ref, open_surf_ref, open_mass_ref):
    depth = depth_ref[...]
    bed = bed_ref[...]
    mass = mass_ref[...]
    cond = cond_ref[...]
    opened = wet_ref[...].astype(jnp.float32)
    surface = depth + bed
    tile_y, tile_x = depth.shape
    own = (surface, mass, cond, opened)
    row_id = lax.broadcasted_iota(jnp.int32, (tile_y, tile_x), 0)
    col_id = lax.broadcasted_iota(jnp.int32, (tile_y, tile_x), 1)
    rows = rows_ref[...]
    cols = cols_ref[...]

    def coeff(c_i, o_i, c_j, o_j):
        return 0.5 * (c_i + c_j) * o_i * o_j

    def ahead(field, axis):
        value = own[field]
        if axis == 0:
            return jnp.where(row_id == tile_y - 1, rows[4 + field : 5 + field, :], pltpu.roll(value, tile_y - 1, 0))
        return jnp.where(col_id == tile_x - 1, cols[:, 4 + field : 5 + field], pltpu.roll(value, tile_x - 1, 1))

    flux = []
    for axis in (0, 1):
        a = coeff(cond, opened, ahead(2, axis), ahead(3, axis))
        flux.append((a * (ahead(0, axis) - surface), a * (ahead(1, axis) - mass)))

    top = rows[0:4, :]
    left = cols[:, 0:4]
    a_top = coeff(cond[0:1, :], opened[0:1, :], top[2:3, :], top[3:4, :])
    a_left = coeff(cond[:, 0:1], opened[:, 0:1], left[:, 2:3], left[:, 3:4])
    edge_y = (a_top * (top[0:1, :] - surface[0:1, :]), a_top * (top[1:2, :] - mass[0:1, :]))
    edge_x = (a_left * (left[:, 0:1] - surface[:, 0:1]), a_left * (left[:, 1:2] - mass[:, 0:1]))

    def behind(k):
        from_y = jnp.where(row_id == 0, edge_y[k], -pltpu.roll(flux[0][k], 1, 0))
        from_x = jnp.where(col_id == 0, edge_x[k], -pltpu.roll(flux[1][k], 1, 1))
        return from_y, from_x

    gains = []
    for k in (0, 1):
        from_y, from_x = behind(k)
        gains.append(((flux[0][k] + from_y) + flux[1][k]) + from_x)
    depth1 = depth + gains[0]
    mass1 = (mass + gains[1]) * jnp.exp(-settle_ref[...])
    depth1_ref[...] = depth1
    mass1_ref[...] = mass1
    per_row = tile_x // 128
    surface1 = depth1 + bed
    for j in range(per_row):
        lanes = slice(j * 128, (j + 1) * 128)
        rows_j = pl.ds(j, tile_y, stride=per_row)
        open_j = opened[:, lanes]
        open_surf_ref[rows_j, :] = open_j * surface1[:, lanes]
        open_mass_ref[rows_j, :] = open_j * mass1[:, lanes]


def smooth_reach(values):
    left = jnp.concatenate([values[:, :1], values[:, :-1]], axis=1)
    right = jnp.concatenate([values[:, 1:], values[:, -1:]], axis=1)
    return values + 0.25 * (left - 2.0 * values + right)


def body(
    depth,
    bed,
    mass,
    conduct,
    settle,
    wet,
    link_block,
    link_owner,
    link_reach,
    link_coef,
    chan_phase,
    chan_conc,
    chan_area,
):
    tile_y, tile_x = depth.shape
    opened = wet.astype(jnp.float32)

    stacked = jnp.stack([depth + bed, mass, conduct, opened])
    top, bottom = halo_pair(stacked[:, tile_y - 1, :], stacked[:, 0, :], "row")
    left, right = halo_pair(stacked[:, :, tile_x - 1], stacked[:, :, 0], "col")
    rows = jnp.concatenate([top, bottom], axis=0)
    cols = jnp.concatenate([left, right], axis=0).T
    tile = jax.ShapeDtypeStruct((tile_y, tile_x), jnp.float32)
    vmem = pl.BlockSpec(memory_space=pltpu.VMEM)
    blocks = tile_y * tile_x // 128
    block_rows = jax.ShapeDtypeStruct((blocks, 128), jnp.float32)
    depth1, mass1, open_surf, open_mass = pl.pallas_call(
        stencil_kernel,
        out_shape=[tile, tile] + [block_rows] * 2,
        in_specs=[vmem] * 8,
        out_specs=[vmem] * 4,
        cost_estimate=pl.CostEstimate(
            flops=60 * tile_y * tile_x, transcendentals=tile_y * tile_x, bytes_accessed=40 * tile_y * tile_x
        ),
    )(depth, bed, mass, conduct, settle, wet, rows, cols)

    n_row = lax.axis_size("row")
    n_col = lax.axis_size("col")
    devices = n_row * n_col
    links_here = link_owner.shape[0]
    slot_cap = max(2, 2 * links_here // devices)
    target = link_owner[:, 0]
    owner_hot = (target[:, None] == jnp.arange(devices, dtype=jnp.int32)[None, :]).astype(jnp.int32)
    ranking = jnp.sum((jnp.cumsum(owner_hot, axis=0) - 1) * owner_hot, axis=1)
    slot_of = target * slot_cap + ranking
    slot_ids = jnp.arange(devices * slot_cap, dtype=jnp.int32)
    slot_hit = slot_of[None, :] == slot_ids[:, None]
    slot_block = jnp.max(jnp.where(slot_hit, link_block[None, :], -1), axis=1)
    block_ids = jnp.arange(blocks, dtype=jnp.int32)
    slot_hot = (slot_block[:, None] == block_ids[None, :]).astype(jnp.float32)
    coefs = jnp.maximum(jnp.max(jnp.where(slot_hit, link_coef[None, :], -1.0), axis=1), 0.0)
    payload = coefs[:, None] * jnp.dot(
        slot_hot, jnp.concatenate([open_surf, open_mass], axis=1), precision=lax.Precision.HIGH
    )
    tags = jnp.max(jnp.where(slot_hit, link_reach[None, :].astype(jnp.float32), -1.0), axis=1)
    meta = jnp.concatenate(
        [tags.reshape(devices, slot_cap), coefs.reshape(devices, slot_cap),
         jnp.zeros((devices, 128 - 2 * slot_cap), jnp.float32)],
        axis=1,
    )
    outgoing = jnp.concatenate([payload.reshape(devices, 2 * slot_cap * 128), meta], axis=1)
    arrived = lax.all_to_all(outgoing, ("row", "col"), split_axis=0, concat_axis=0, tiled=True)
    got = arrived[:, : 2 * slot_cap * 128].reshape(devices * slot_cap, 256)
    arrived_tags = arrived[:, 2 * slot_cap * 128 : 2 * slot_cap * 128 + slot_cap].reshape(devices * slot_cap)
    arrived_coef = arrived[:, 2 * slot_cap * 128 + slot_cap : 2 * slot_cap * 128 + 2 * slot_cap].reshape(
        devices * slot_cap
    )
    got_ws = got[:, :128]
    got_wm = got[:, 128:]
    got_w = jnp.where(got_wm > 0.0, arrived_coef[:, None], 0.0)
    reach_dev = chan_phase.shape[0]
    reach_hot = (arrived_tags[None, :] == jnp.arange(reach_dev, dtype=jnp.float32)[:, None]).astype(
        jnp.float32
    )
    totals = jnp.dot(
        reach_hot, jnp.concatenate([got_ws, got_wm, got_w], axis=1), precision=lax.Precision.HIGHEST
    )
    inflow = totals[:, :128]
    sediment = totals[:, 128:256]
    wet_sum = totals[:, 256:]
    phase_new = (chan_area * chan_phase + inflow) / (chan_area + wet_sum)
    conc_new = (chan_area * chan_conc + sediment) / (chan_area + wet_sum)
    phase_out = smooth_reach(phase_new)
    conc_out = smooth_reach(conc_new)
    reply = jnp.dot(
        reach_hot.T, jnp.concatenate([phase_out, conc_out], axis=1), precision=lax.Precision.HIGH
    )
    answered = lax.all_to_all(
        reply.reshape(devices, slot_cap, 256),
        ("row", "col"),
        split_axis=0,
        concat_axis=0,
        tiled=True,
    )
    own_rows = answered.reshape(devices * slot_cap, 256)
    slot_read = jnp.maximum(slot_block, 0)
    surf_rows = (depth1 + bed).reshape(blocks, 128)[slot_read]
    mass_rows = mass1.reshape(blocks, 128)[slot_read]
    weight = coefs[:, None] * opened.reshape(blocks, 128)[slot_read]
    applied = jnp.concatenate(
        [
            0.5 * weight * (own_rows[:, :128] - surf_rows),
            0.5 * weight * (own_rows[:, 128:] - mass_rows),
        ],
        axis=1,
    )
    per_row = tile_x // 128
    row_ids = jnp.arange(tile_y, dtype=jnp.int32)[:, None]
    column_ids = jnp.arange(per_row, dtype=jnp.int32)[:, None, None]
    block_hot = (row_ids[None] * per_row + column_ids == slot_block[None, None, :]).astype(jnp.float32)
    gained = jnp.einsum("jyl,lc->jyc", block_hot, applied, precision=lax.Precision.HIGH)
    depth_out = depth1 + jnp.concatenate([gained[j, :, :128] for j in range(per_row)], axis=1)
    mass_out = mass1 + jnp.concatenate([gained[j, :, 128:] for j in range(per_row)], axis=1)
    return (depth_out, mass_out, phase_out, conc_out)


def solution(mesh):
    return jax.shard_map(
        body,
        mesh=mesh,
        in_specs=(
            P("row", "col"),
            P("row", "col"),
            P("row", "col"),
            P("row", "col"),
            P("row", "col"),
            P("row", "col"),
            P(("row", "col")),
            P(("row", "col"), None),
            P(("row", "col")),
            P(("row", "col")),
            P(("row", "col"), None),
            P(("row", "col"), None),
            P(("row", "col"), None),
        ),
        out_specs=(
            P("row", "col"),
            P("row", "col"),
            P(("row", "col"), None),
            P(("row", "col"), None),
        ),
        check_vma=False,
    )
```

```python
import jax
import jax.numpy as jnp
from jax import lax
from jax.experimental import pallas as pl
from jax.experimental.pallas import tpu as pltpu
from jax.sharding import PartitionSpec as P


def halo_pair(last, first, axis):
    count = lax.axis_size(axis)
    forward = [(i, i + 1) for i in range(count - 1)]
    backward = [(target, source) for source, target in forward]
    return lax.ppermute(last, axis, forward), lax.ppermute(first, axis, backward)


def stencil_kernel(depth_ref, bed_ref, mass_ref, cond_ref, settle_ref, wet_ref, rows_ref, cols_ref,
                   depth1_ref, mass1_ref, open_surf_ref, open_mass_ref):
    depth = depth_ref[...]
    bed = bed_ref[...]
    mass = mass_ref[...]
    cond = cond_ref[...]
    opened = wet_ref[...].astype(jnp.float32)
    surface = depth + bed
    tile_y, tile_x = depth.shape
    own = (surface, mass, cond, opened)
    row_id = lax.broadcasted_iota(jnp.int32, (tile_y, tile_x), 0)
    col_id = lax.broadcasted_iota(jnp.int32, (tile_y, tile_x), 1)
    rows = rows_ref[...]
    cols = cols_ref[...]

    def coeff(c_i, o_i, c_j, o_j):
        return 0.5 * (c_i + c_j) * o_i * o_j

    def ahead(field, axis):
        value = own[field]
        if axis == 0:
            return jnp.where(row_id == tile_y - 1, rows[4 + field : 5 + field, :], pltpu.roll(value, tile_y - 1, 0))
        return jnp.where(col_id == tile_x - 1, cols[:, 4 + field : 5 + field], pltpu.roll(value, tile_x - 1, 1))

    flux = []
    for axis in (0, 1):
        a = coeff(cond, opened, ahead(2, axis), ahead(3, axis))
        flux.append((a * (ahead(0, axis) - surface), a * (ahead(1, axis) - mass)))

    top = rows[0:4, :]
    left = cols[:, 0:4]
    a_top = coeff(cond[0:1, :], opened[0:1, :], top[2:3, :], top[3:4, :])
    a_left = coeff(cond[:, 0:1], opened[:, 0:1], left[:, 2:3], left[:, 3:4])
    edge_y = (a_top * (top[0:1, :] - surface[0:1, :]), a_top * (top[1:2, :] - mass[0:1, :]))
    edge_x = (a_left * (left[:, 0:1] - surface[:, 0:1]), a_left * (left[:, 1:2] - mass[:, 0:1]))

    def behind(k):
        from_y = jnp.where(row_id == 0, edge_y[k], -pltpu.roll(flux[0][k], 1, 0))
        from_x = jnp.where(col_id == 0, edge_x[k], -pltpu.roll(flux[1][k], 1, 1))
        return from_y, from_x

    gains = []
    for k in (0, 1):
        from_y, from_x = behind(k)
        gains.append(((flux[0][k] + from_y) + flux[1][k]) + from_x)
    depth1 = depth + gains[0]
    mass1 = (mass + gains[1]) * jnp.exp(-settle_ref[...])
    depth1_ref[...] = depth1
    mass1_ref[...] = mass1
    per_row = tile_x // 128
    surface1 = depth1 + bed
    for j in range(per_row):
        lanes = slice(j * 128, (j + 1) * 128)
        rows_j = pl.ds(j, tile_y, stride=per_row)
        open_j = opened[:, lanes]
        open_surf_ref[rows_j, :] = open_j * surface1[:, lanes]
        open_mass_ref[rows_j, :] = open_j * mass1[:, lanes]


def smooth_reach(values):
    left = jnp.concatenate([values[:, :1], values[:, :-1]], axis=1)
    right = jnp.concatenate([values[:, 1:], values[:, -1:]], axis=1)
    return values + 0.25 * (left - 2.0 * values + right)


def body(
    depth,
    bed,
    mass,
    conduct,
    settle,
    wet,
    link_block,
    link_owner,
    link_reach,
    link_coef,
    chan_phase,
    chan_conc,
    chan_area,
):
    tile_y, tile_x = depth.shape
    opened = wet.astype(jnp.float32)

    stacked = jnp.stack([depth + bed, mass, conduct, opened])
    top, bottom = halo_pair(stacked[:, tile_y - 1, :], stacked[:, 0, :], "row")
    left, right = halo_pair(stacked[:, :, tile_x - 1], stacked[:, :, 0], "col")
    rows = jnp.concatenate([top, bottom], axis=0)
    cols = jnp.concatenate([left, right], axis=0).T
    tile = jax.ShapeDtypeStruct((tile_y, tile_x), jnp.float32)
    vmem = pl.BlockSpec(memory_space=pltpu.VMEM)
    blocks = tile_y * tile_x // 128
    block_rows = jax.ShapeDtypeStruct((blocks, 128), jnp.float32)
    depth1, mass1, open_surf, open_mass = pl.pallas_call(
        stencil_kernel,
        out_shape=[tile, tile] + [block_rows] * 2,
        in_specs=[vmem] * 8,
        out_specs=[vmem] * 4,
        cost_estimate=pl.CostEstimate(
            flops=60 * tile_y * tile_x, transcendentals=tile_y * tile_x, bytes_accessed=40 * tile_y * tile_x
        ),
    )(depth, bed, mass, conduct, settle, wet, rows, cols)

    n_row = lax.axis_size("row")
    n_col = lax.axis_size("col")
    devices = n_row * n_col
    links_here = link_owner.shape[0]
    slot_cap = max(2, 2 * links_here // devices)
    target = link_owner[:, 0]
    owner_hot = (target[:, None] == jnp.arange(devices, dtype=jnp.int32)[None, :]).astype(jnp.int32)
    ranking = jnp.sum((jnp.cumsum(owner_hot, axis=0) - 1) * owner_hot, axis=1)
    slot_of = target * slot_cap + ranking
    slot_ids = jnp.arange(devices * slot_cap, dtype=jnp.int32)
    slot_hit = slot_of[None, :] == slot_ids[:, None]
    slot_block = jnp.max(jnp.where(slot_hit, link_block[None, :], -1), axis=1)
    block_ids = jnp.arange(blocks, dtype=jnp.int32)
    slot_hot = (slot_block[:, None] == block_ids[None, :]).astype(jnp.float32)
    coefs = jnp.maximum(jnp.max(jnp.where(slot_hit, link_coef[None, :], -1.0), axis=1), 0.0)
    payload = coefs[:, None] * jnp.dot(
        slot_hot, jnp.concatenate([open_surf, open_mass], axis=1), precision=lax.Precision.HIGH
    )
    tags = jnp.max(jnp.where(slot_hit, link_reach[None, :].astype(jnp.float32), -1.0), axis=1)
    meta = jnp.concatenate(
        [tags.reshape(devices, slot_cap), coefs.reshape(devices, slot_cap),
         jnp.zeros((devices, 128 - 2 * slot_cap), jnp.float32)],
        axis=1,
    )
    outgoing = jnp.concatenate([payload.reshape(devices, 2 * slot_cap * 128), meta], axis=1)
    arrived = lax.all_to_all(outgoing, ("row", "col"), split_axis=0, concat_axis=0, tiled=True)
    got = arrived[:, : 2 * slot_cap * 128].reshape(devices * slot_cap, 256)
    arrived_tags = arrived[:, 2 * slot_cap * 128 : 2 * slot_cap * 128 + slot_cap].reshape(devices * slot_cap)
    arrived_coef = arrived[:, 2 * slot_cap * 128 + slot_cap : 2 * slot_cap * 128 + 2 * slot_cap].reshape(
        devices * slot_cap
    )
    got_ws = got[:, :128]
    got_wm = got[:, 128:]
    got_w = jnp.where(got_wm > 0.0, arrived_coef[:, None], 0.0)
    reach_dev = chan_phase.shape[0]
    reach_hot = (arrived_tags[None, :] == jnp.arange(reach_dev, dtype=jnp.float32)[:, None]).astype(
        jnp.float32
    )
    totals = jnp.dot(
        reach_hot, jnp.concatenate([got_ws, got_wm, got_w], axis=1), precision=lax.Precision.HIGH
    )
    inflow = totals[:, :128]
    sediment = totals[:, 128:256]
    wet_sum = totals[:, 256:]
    phase_new = (chan_area * chan_phase + inflow) / (chan_area + wet_sum)
    conc_new = (chan_area * chan_conc + sediment) / (chan_area + wet_sum)
    phase_out = smooth_reach(phase_new)
    conc_out = smooth_reach(conc_new)
    reply = jnp.dot(
        reach_hot.T, jnp.concatenate([phase_out, conc_out], axis=1), precision=lax.Precision.HIGH
    )
    answered = lax.all_to_all(
        reply.reshape(devices, slot_cap, 256),
        ("row", "col"),
        split_axis=0,
        concat_axis=0,
        tiled=True,
    )
    own_rows = jnp.dot(
        slot_hit.T.astype(jnp.float32), answered.reshape(devices * slot_cap, 256), precision=lax.Precision.HIGH
    )
    surf_rows = (depth1 + bed).reshape(blocks, 128)[link_block]
    mass_rows = mass1.reshape(blocks, 128)[link_block]
    weight = link_coef[:, None] * opened.reshape(blocks, 128)[link_block]
    applied = jnp.concatenate(
        [
            0.5 * weight * (own_rows[:, :128] - surf_rows),
            0.5 * weight * (own_rows[:, 128:] - mass_rows),
        ],
        axis=1,
    )
    per_row = tile_x // 128
    row_ids = jnp.arange(tile_y, dtype=jnp.int32)[:, None]
    column_ids = jnp.arange(per_row, dtype=jnp.int32)[:, None, None]
    block_hot = (row_ids[None] * per_row + column_ids == link_block[None, None, :]).astype(jnp.float32)
    gained = jnp.einsum("jyl,lc->jyc", block_hot, applied, precision=lax.Precision.HIGH)
    depth_out = depth1 + jnp.concatenate([gained[j, :, :128] for j in range(per_row)], axis=1)
    mass_out = mass1 + jnp.concatenate([gained[j, :, 128:] for j in range(per_row)], axis=1)
    return (depth_out, mass_out, phase_out, conc_out)


def solution(mesh):
    return jax.shard_map(
        body,
        mesh=mesh,
        in_specs=(
            P("row", "col"),
            P("row", "col"),
            P("row", "col"),
            P("row", "col"),
            P("row", "col"),
            P("row", "col"),
            P(("row", "col")),
            P(("row", "col"), None),
            P(("row", "col")),
            P(("row", "col")),
            P(("row", "col"), None),
            P(("row", "col"), None),
            P(("row", "col"), None),
        ),
        out_specs=(
            P("row", "col"),
            P("row", "col"),
            P(("row", "col"), None),
            P(("row", "col"), None),
        ),
        check_vma=False,
    )
```

```python
import jax
import jax.numpy as jnp
from jax import lax
from jax.experimental import pallas as pl
from jax.experimental.pallas import tpu as pltpu
from jax.sharding import PartitionSpec as P


def halo_pair(last, first, axis):
    count = lax.axis_size(axis)
    forward = [(i, i + 1) for i in range(count - 1)]
    backward = [(target, source) for source, target in forward]
    return lax.ppermute(last, axis, forward), lax.ppermute(first, axis, backward)


def stencil_kernel(depth_ref, bed_ref, mass_ref, cond_ref, settle_ref, wet_ref, rows_ref, cols_ref,
                   depth1_ref, mass1_ref, open_surf_ref, open_mass_ref):
    depth = depth_ref[...]
    bed = bed_ref[...]
    mass = mass_ref[...]
    cond = cond_ref[...]
    opened = wet_ref[...].astype(jnp.float32)
    surface = depth + bed
    tile_y, tile_x = depth.shape
    own = (surface, mass, cond, opened)
    row_id = lax.broadcasted_iota(jnp.int32, (tile_y, tile_x), 0)
    col_id = lax.broadcasted_iota(jnp.int32, (tile_y, tile_x), 1)
    rows = rows_ref[...]
    cols = cols_ref[...]

    def coeff(c_i, o_i, c_j, o_j):
        return 0.5 * (c_i + c_j) * o_i * o_j

    def ahead(field, axis):
        value = own[field]
        if axis == 0:
            return jnp.where(row_id == tile_y - 1, rows[4 + field : 5 + field, :], pltpu.roll(value, tile_y - 1, 0))
        return jnp.where(col_id == tile_x - 1, cols[:, 4 + field : 5 + field], pltpu.roll(value, tile_x - 1, 1))

    flux = []
    for axis in (0, 1):
        a = coeff(cond, opened, ahead(2, axis), ahead(3, axis))
        flux.append((a * (ahead(0, axis) - surface), a * (ahead(1, axis) - mass)))

    top = rows[0:4, :]
    left = cols[:, 0:4]
    a_top = coeff(cond[0:1, :], opened[0:1, :], top[2:3, :], top[3:4, :])
    a_left = coeff(cond[:, 0:1], opened[:, 0:1], left[:, 2:3], left[:, 3:4])
    edge_y = (a_top * (top[0:1, :] - surface[0:1, :]), a_top * (top[1:2, :] - mass[0:1, :]))
    edge_x = (a_left * (left[:, 0:1] - surface[:, 0:1]), a_left * (left[:, 1:2] - mass[:, 0:1]))

    def behind(k):
        from_y = jnp.where(row_id == 0, edge_y[k], -pltpu.roll(flux[0][k], 1, 0))
        from_x = jnp.where(col_id == 0, edge_x[k], -pltpu.roll(flux[1][k], 1, 1))
        return from_y, from_x

    gains = []
    for k in (0, 1):
        from_y, from_x = behind(k)
        gains.append(((flux[0][k] + from_y) + flux[1][k]) + from_x)
    depth1 = depth + gains[0]
    mass1 = (mass + gains[1]) * jnp.exp(-settle_ref[...])
    depth1_ref[...] = depth1
    mass1_ref[...] = mass1
    per_row = tile_x // 128
    surface1 = depth1 + bed
    for j in range(per_row):
        lanes = slice(j * 128, (j + 1) * 128)
        rows_j = pl.ds(j, tile_y, stride=per_row)
        open_j = opened[:, lanes]
        open_surf_ref[rows_j, :] = open_j * surface1[:, lanes]
        open_mass_ref[rows_j, :] = open_j * mass1[:, lanes]


def smooth_reach(values):
    left = jnp.concatenate([values[:, :1], values[:, :-1]], axis=1)
    right = jnp.concatenate([values[:, 1:], values[:, -1:]], axis=1)
    return values + 0.25 * (left - 2.0 * values + right)


def body(
    depth,
    bed,
    mass,
    conduct,
    settle,
    wet,
    link_block,
    link_owner,
    link_reach,
    link_coef,
    chan_phase,
    chan_conc,
    chan_area,
):
    tile_y, tile_x = depth.shape
    opened = wet.astype(jnp.float32)

    stacked = jnp.stack([depth + bed, mass, conduct, opened])
    top, bottom = halo_pair(stacked[:, tile_y - 1, :], stacked[:, 0, :], "row")
    left, right = halo_pair(stacked[:, :, tile_x - 1], stacked[:, :, 0], "col")
    rows = jnp.concatenate([top, bottom], axis=0)
    cols = jnp.concatenate([left, right], axis=0).T
    tile = jax.ShapeDtypeStruct((tile_y, tile_x), jnp.float32)
    vmem = pl.BlockSpec(memory_space=pltpu.VMEM)
    blocks = tile_y * tile_x // 128
    block_rows = jax.ShapeDtypeStruct((blocks, 128), jnp.float32)
    depth1, mass1, open_surf, open_mass = pl.pallas_call(
        stencil_kernel,
        out_shape=[tile, tile] + [block_rows] * 2,
        in_specs=[vmem] * 8,
        out_specs=[vmem] * 4,
        cost_estimate=pl.CostEstimate(
            flops=60 * tile_y * tile_x, transcendentals=tile_y * tile_x, bytes_accessed=40 * tile_y * tile_x
        ),
    )(depth, bed, mass, conduct, settle, wet, rows, cols)

    n_row = lax.axis_size("row")
    n_col = lax.axis_size("col")
    devices = n_row * n_col
    links_here = link_owner.shape[0]
    slot_cap = max(2, 2 * links_here // devices)
    target = link_owner[:, 0]
    owner_hot = (target[:, None] == jnp.arange(devices, dtype=jnp.int32)[None, :]).astype(jnp.int32)
    ranking = jnp.sum((jnp.cumsum(owner_hot, axis=0) - 1) * owner_hot, axis=1)
    slot_of = target * slot_cap + ranking
    slot_ids = jnp.arange(devices * slot_cap, dtype=jnp.int32)
    slot_hit = slot_of[None, :] == slot_ids[:, None]
    slot_block = jnp.max(jnp.where(slot_hit, link_block[None, :], -1), axis=1)
    block_ids = jnp.arange(blocks, dtype=jnp.int32)
    slot_hot = (slot_block[:, None] == block_ids[None, :]).astype(jnp.float32)
    coefs = jnp.maximum(jnp.max(jnp.where(slot_hit, link_coef[None, :], -1.0), axis=1), 0.0)
    payload = coefs[:, None] * jnp.dot(
        slot_hot, jnp.concatenate([open_surf, open_mass], axis=1), precision=lax.Precision.HIGH
    )
    tags = jnp.max(jnp.where(slot_hit, link_reach[None, :].astype(jnp.float32), -1.0), axis=1)
    meta = jnp.concatenate(
        [tags.reshape(devices, slot_cap), coefs.reshape(devices, slot_cap),
         jnp.zeros((devices, 128 - 2 * slot_cap), jnp.float32)],
        axis=1,
    )
    outgoing = jnp.concatenate([payload.reshape(devices, 2 * slot_cap * 128), meta], axis=1)
    arrived = lax.all_to_all(outgoing, ("row", "col"), split_axis=0, concat_axis=0, tiled=True)
    got = arrived[:, : 2 * slot_cap * 128].reshape(devices * slot_cap, 256)
    arrived_tags = arrived[:, 2 * slot_cap * 128 : 2 * slot_cap * 128 + slot_cap].reshape(devices * slot_cap)
    arrived_coef = arrived[:, 2 * slot_cap * 128 + slot_cap : 2 * slot_cap * 128 + 2 * slot_cap].reshape(
        devices * slot_cap
    )
    got_ws = got[:, :128]
    got_wm = got[:, 128:]
    got_w = jnp.where(got_wm > 0.0, arrived_coef[:, None], 0.0)
    reach_dev = chan_phase.shape[0]
    reach_hot = (arrived_tags[None, :] == jnp.arange(reach_dev, dtype=jnp.float32)[:, None]).astype(
        jnp.float32
    )
    totals = jnp.dot(
        reach_hot, jnp.concatenate([got_ws, got_wm, got_w], axis=1), precision=lax.Precision.HIGH
    )
    inflow = totals[:, :128]
    sediment = totals[:, 128:256]
    wet_sum = totals[:, 256:]
    phase_new = (chan_area * chan_phase + inflow) / (chan_area + wet_sum)
    conc_new = (chan_area * chan_conc + sediment) / (chan_area + wet_sum)
    phase_out = smooth_reach(phase_new)
    conc_out = smooth_reach(conc_new)
    reply = jnp.dot(
        reach_hot.T, jnp.concatenate([phase_out, conc_out], axis=1), precision=lax.Precision.HIGH
    )
    answered = lax.all_to_all(
        reply.reshape(devices, slot_cap, 256),
        ("row", "col"),
        split_axis=0,
        concat_axis=0,
        tiled=True,
    )
    own_rows = answered.reshape(devices * slot_cap, 256)[slot_of]
    surf_rows = (depth1 + bed).reshape(blocks, 128)[link_block]
    mass_rows = mass1.reshape(blocks, 128)[link_block]
    weight = link_coef[:, None] * opened.reshape(blocks, 128)[link_block]
    applied = jnp.concatenate(
        [
            0.5 * weight * (own_rows[:, :128] - surf_rows),
            0.5 * weight * (own_rows[:, 128:] - mass_rows),
        ],
        axis=1,
    )
    per_row = tile_x // 128
    row_ids = jnp.arange(tile_y, dtype=jnp.int32)[:, None]
    column_ids = jnp.arange(per_row, dtype=jnp.int32)[:, None, None]
    block_hot = (row_ids[None] * per_row + column_ids == link_block[None, None, :]).astype(jnp.float32)
    gained = jnp.einsum("jyl,lc->jyc", block_hot, applied, precision=lax.Precision.HIGH)
    depth_out = depth1 + jnp.concatenate([gained[j, :, :128] for j in range(per_row)], axis=1)
    mass_out = mass1 + jnp.concatenate([gained[j, :, 128:] for j in range(per_row)], axis=1)
    return (depth_out, mass_out, phase_out, conc_out)


def solution(mesh):
    return jax.shard_map(
        body,
        mesh=mesh,
        in_specs=(
            P("row", "col"),
            P("row", "col"),
            P("row", "col"),
            P("row", "col"),
            P("row", "col"),
            P("row", "col"),
            P(("row", "col")),
            P(("row", "col"), None),
            P(("row", "col")),
            P(("row", "col")),
            P(("row", "col"), None),
            P(("row", "col"), None),
            P(("row", "col"), None),
        ),
        out_specs=(
            P("row", "col"),
            P("row", "col"),
            P(("row", "col"), None),
            P(("row", "col"), None),
        ),
        check_vma=False,
    )
```
